256 devices in a mesh: seq: 64 (over y, z, core), tp: 4 (over x).
Axes of the slice: x: 4, y: 4, z: 8, core: 2. Of those that a mesh axis runs over, the one named last changes fastest.
Arguments:
- tier_source_concatenated: bfloat16 [8192, 2048], P('seq', 'tp'), may hold values from -6 to 6
- prompt_sizes_ordered: int32 [4], replicated, may hold values from 1 to 4096, 8192 in all
- tier_standardize_scale: float32 [2048], replicated, may hold values from 0.1 to 1.9
- tier_standardize_offset: float32 [2048], replicated, may hold values from -3 to 3
- previous_item_mixers: float32 [5, 2048], replicated, may hold values from 0 to 1
- mapping_matrices_pile: bfloat16 [4, 2048, 2048], P(None, None, 'tp'), may hold values from -0.125 to 0.125
- fading_narrow_left: bfloat16 [2048, 64], replicated, may hold values from -0.125 to 0.125
- fading_narrow_right: bfloat16 [64, 2048], P(None, 'tp'), may hold values from -0.75 to 0.75
- feature_fading_baseline: float32 [2048], P('tp'), may hold values from 5e-05 to 0.04
- diagonal_boost_coefficient: float32 [2048], P('tp'), may hold values from -4 to 4
- cluster_standardize_scale: float32 [2048], P('tp'), may hold values from 0.1 to 1.9
- cluster_standardize_offset: float32 [2048], P('tp'), may hold values from -3 to 3
- emitted_mapping_matrix: bfloat16 [2048, 2048], P('tp'), may hold values from -0.125 to 0.125
Outputs:
- hidden_out: bfloat16 [8192, 2048], P('seq', 'tp')
The draws below stay inside these ranges and needn't reach their ends.
Inputs may be any that keep to these rules, and one draw needn't show every extreme that they name: `prompt_sizes_ordered`: the prompt lengths sum to 8192, and the longest is exactly 4096.
All inputs are finite; a program needn't handle non-finite values.
Results may differ from the reference program's by a relative error of at most 0.025.
Values may be sent and summed in bfloat16 or wider, within the bound.
No kernel may reach another device: no remote copies, remote signals or barrier semaphores. Data moves between devices by JAX's collectives and lax.ppermute only.
A program may use at most 128 MiB of HBM per device.

```python
import math
import jax
import jax.numpy as jnp
import numpy as np
from jax import lax

EMBEDDING_SIZE = 2048
CHANNELS_ONE_HEAD = 64
DL = 64
TOKENS = 8192
REQUESTS = 4
MAX_LEN = 4096


def steps_of(stream_key, extent, shards, smallest, high):
    level = 1.0
    for axis_at, blocks in shards:
        steps = jax.random.uniform(jax.random.fold_in(jax.random.fold_in(stream_key, 6), axis_at), (blocks,), jnp.float32, smallest / len(shards), high / len(shards))
        level = level * jnp.repeat(jnp.exp(steps), extent[axis_at] // blocks).reshape((-1,) + (1,) * (len(extent) - 1 - axis_at))
    return level


def profile(count, total, limit, skew):
    weights = [(1 << 20) // math.isqrt(standing ** skew) + 1 for standing in range(2, count + 1)]
    rest, holding = total - limit - (count - 1), [1] * (count - 1)
    while rest > 0:
        candidates = [i for i in range(count - 1) if holding[i] < limit]
        mass, remaining = sum([weights[i] for i in candidates]), rest
        for i in candidates:
            addition = min(limit - holding[i], max(1, remaining * weights[i] // mass), rest)
            holding[i] = holding[i] + addition
            rest = rest - addition
    return np.array([limit] + holding)


def uneven_parts(own_key, count, total, bound, slope):
    if count == 2:
        one = jax.random.randint(own_key, (), max(1, total - bound), min(bound, total - 1) + 1)
        return jnp.stack([one, total - one])
    tallies = jnp.asarray(profile(count, total, bound, slope), jnp.int32)
    pairs = (count - 1) // 2
    source_of, taker = tallies[1:1 + 2 * pairs:2], tallies[2:2 + 2 * pairs:2]
    margin = jnp.minimum(source_of - 1, bound - taker)
    shifted = jax.random.randint(jax.random.fold_in(own_key, 1), (pairs,), 0, 1 << 20) % (margin + 1)
    tallies = tallies.at[1:1 + 2 * pairs:2].set(source_of - shifted).at[2:2 + 2 * pairs:2].set(taker + shifted)
    return tallies[jax.random.permutation(jax.random.fold_in(own_key, 2), count)]


def normal_values(stream_key, extent, deviation, most, split=(), kind=jnp.bfloat16):
    level = steps_of(stream_key, extent, split, -0.22, 0.18) if split else 1.0
    result = jax.random.normal(stream_key, extent, jnp.float32) * deviation * level
    return jnp.minimum(jnp.maximum(result, -most), most).astype(kind)


def setup_inputs(seed: int = 0) -> dict:
    streams_of = jax.random.split(jax.random.key(seed), 14)
    tier_source_concatenated = normal_values(streams_of[0], (TOKENS, EMBEDDING_SIZE), 1.0, 6.0, ((0, 64), (1, 4)))
    prompt_sizes_ordered = uneven_parts(streams_of[1], REQUESTS, TOKENS, MAX_LEN, 2).astype(jnp.int32)
    tier_standardize_scale = jnp.clip(1.0 + 0.18 * jax.random.normal(streams_of[2], (EMBEDDING_SIZE,), jnp.float32), 0.1, 1.9)
    tier_standardize_offset = normal_values(streams_of[3], (EMBEDDING_SIZE,), 0.5, 3.0, (), jnp.float32)
    previous_item_mixers = jnp.clip(jax.random.uniform(streams_of[4], (5, EMBEDDING_SIZE), jnp.float32, 0.0, 1.0), 0.0, 1.0)
    mapping_matrices_pile = normal_values(streams_of[5], (4, EMBEDDING_SIZE, EMBEDDING_SIZE), EMBEDDING_SIZE ** -0.5, 0.125, ((2, 4),))
    fading_narrow_left = normal_values(streams_of[6], (EMBEDDING_SIZE, DL), EMBEDDING_SIZE ** -0.5, 0.125)
    fading_narrow_right = normal_values(streams_of[7], (DL, EMBEDDING_SIZE), DL ** -0.5, 0.75, ((1, 4),))
    feature_fading_baseline = jnp.clip(jnp.exp(math.log(0.04) - 6.684612 * jax.random.uniform(streams_of[8], (EMBEDDING_SIZE,), jnp.float32) ** steps_of(streams_of[8], (EMBEDDING_SIZE,), ((0, 4),), -0.2, 0.2)), 4.999999873689376e-05, 0.04)
    diagonal_boost_coefficient = normal_values(streams_of[9], (EMBEDDING_SIZE,), 1.0, 4.0, ((0, 4),), jnp.float32)
    cluster_standardize_scale = jnp.clip(1.0 + 0.18 * jax.random.normal(streams_of[10], (EMBEDDING_SIZE,), jnp.float32), 0.1, 1.9)
    cluster_standardize_offset = normal_values(streams_of[11], (EMBEDDING_SIZE,), 0.5, 3.0, ((0, 4),), jnp.float32)
    emitted_mapping_matrix = normal_values(streams_of[12], (EMBEDDING_SIZE, EMBEDDING_SIZE), EMBEDDING_SIZE ** -0.5, 0.125, ((0, 4),))
    return {"tier_source_concatenated": tier_source_concatenated, "prompt_sizes_ordered": prompt_sizes_ordered, "tier_standardize_scale": tier_standardize_scale, "tier_standardize_offset": tier_standardize_offset, "previous_item_mixers": previous_item_mixers, "mapping_matrices_pile": mapping_matrices_pile, "fading_narrow_left": fading_narrow_left, "fading_narrow_right": fading_narrow_right, "feature_fading_baseline": feature_fading_baseline, "diagonal_boost_coefficient": diagonal_boost_coefficient, "cluster_standardize_scale": cluster_standardize_scale, "cluster_standardize_offset": cluster_standardize_offset, "emitted_mapping_matrix": emitted_mapping_matrix}


def layer_norm(rows, gain, bias, eps):
    mean = lax.optimization_barrier(jnp.mean(rows, axis=-1, keepdims=True))
    centred = rows - mean
    spread = lax.optimization_barrier(jnp.mean(centred * centred, axis=-1, keepdims=True))
    return centred * lax.rsqrt(spread + eps) * gain + bias

def reference(tier_source_concatenated, prompt_sizes_ordered, tier_standardize_scale, tier_standardize_offset, previous_item_mixers, mapping_matrices_pile, fading_narrow_left, fading_narrow_right, feature_fading_baseline, diagonal_boost_coefficient, cluster_standardize_scale, cluster_standardize_offset, emitted_mapping_matrix):
    total = tier_source_concatenated.shape[0]
    width = tier_source_concatenated.shape[1]
    mixing_values_divided = width // CHANNELS_ONE_HEAD
    first = (jnp.cumsum(prompt_sizes_ordered) - prompt_sizes_ordered).astype(jnp.int32)
    position = jnp.arange(total, dtype=jnp.int32)
    is_start = jnp.any(position[:, None] == first[None, :], axis=1)
    normed = layer_norm(tier_source_concatenated.astype(jnp.float32), tier_standardize_scale, tier_standardize_offset, 1e-05).astype(jnp.bfloat16)
    previous = jnp.concatenate([jnp.zeros((1, width), jnp.bfloat16), normed[:-1]], axis=0)
    previous = jnp.where(is_start[:, None], jnp.zeros_like(previous), previous)
    base = normed.astype(jnp.float32)
    delta = previous.astype(jnp.float32) - base
    outputs = []
    for index in range(4):
        shifted_blend = (base + delta * previous_item_mixers[index][None, :]).astype(jnp.bfloat16)
        outputs.append(jnp.dot(shifted_blend, mapping_matrices_pile[index], preferred_element_type=jnp.float32))
    recept = outputs[0].astype(jnp.bfloat16)
    key_rows = outputs[1].astype(jnp.bfloat16)
    value_rows = outputs[2].astype(jnp.bfloat16)
    gate = jax.nn.silu(outputs[3]).astype(jnp.bfloat16)
    decay_shifted_blend = (base + delta * previous_item_mixers[4][None, :]).astype(jnp.bfloat16)
    lowrank_decay_delta = jnp.tanh(jnp.dot(decay_shifted_blend, fading_narrow_left, preferred_element_type=jnp.float32)).astype(jnp.bfloat16)
    decay_logarithm = -feature_fading_baseline[None, :] * jnp.exp(jnp.dot(lowrank_decay_delta, fading_narrow_right, preferred_element_type=jnp.float32))
    r_all = recept.astype(jnp.float32).reshape(total, mixing_values_divided, CHANNELS_ONE_HEAD)
    k_all = key_rows.astype(jnp.float32).reshape(total, mixing_values_divided, CHANNELS_ONE_HEAD)
    v_all = value_rows.astype(jnp.float32).reshape(total, mixing_values_divided, CHANNELS_ONE_HEAD)
    d_all = jnp.exp(decay_logarithm).reshape(total, mixing_values_divided, CHANNELS_ONE_HEAD)
    diagonal_extra_contribution = diagonal_boost_coefficient.reshape(mixing_values_divided, CHANNELS_ONE_HEAD)

    def step(running_recurrence_array, item):
        gating_vector_here, k_t, v_t, d_t, s_t = item
        running_recurrence_array = jnp.where(s_t, jnp.zeros_like(running_recurrence_array), running_recurrence_array)
        query_vector_product = k_t[:, :, None] * v_t[:, None, :]
        level_ultimate_outcome = jnp.einsum('yr,yrk->yk', gating_vector_here, running_recurrence_array + diagonal_extra_contribution[:, :, None] * query_vector_product, precision=lax.Precision.HIGHEST)
        running_recurrence_array = d_t[:, :, None] * running_recurrence_array + query_vector_product
        return (running_recurrence_array, level_ultimate_outcome)
    init = jnp.zeros((mixing_values_divided, CHANNELS_ONE_HEAD, CHANNELS_ONE_HEAD), jnp.float32)
    _, wkv = lax.scan(step, init, (r_all, k_all, v_all, d_all, is_start))
    mean = lax.optimization_barrier(jnp.mean(wkv, axis=-1, keepdims=True))
    centred = wkv - mean
    spread = lax.optimization_barrier(jnp.mean(centred * centred, axis=-1, keepdims=True))
    grouped = (centred * lax.rsqrt(spread + 0.00064)).reshape(total, width) * cluster_standardize_scale + cluster_standardize_offset
    gated = (grouped * gate.astype(jnp.float32)).astype(jnp.bfloat16)
    projected = jnp.dot(gated, emitted_mapping_matrix, preferred_element_type=jnp.float32)
    return (tier_source_concatenated.astype(jnp.float32) + projected).astype(jnp.bfloat16)
```

```python
import jax
import jax.numpy as jnp
from jax import lax
from jax.sharding import PartitionSpec as P

CHANNELS_ONE_HEAD = 64


highest = lax.Precision.HIGHEST


def from_behind(block, axis, distance):
    devices = range(lax.axis_size(axis))
    route = [(i - distance, i) for i in devices if i - distance in devices]
    return lax.ppermute(block, axis, route)


def layer_norm(rows, gain, bias, eps):
    mean = jnp.mean(rows, axis=-1, keepdims=True)
    centred = rows - mean
    spread = jnp.mean(centred * centred, axis=-1, keepdims=True)
    return centred * lax.rsqrt(spread + eps) * gain + bias


def body(
    tier_source_concatenated,
    prompt_sizes_ordered,
    tier_standardize_scale,
    tier_standardize_offset,
    previous_item_mixers,
    mapping_matrices_pile,
    fading_narrow_left,
    fading_narrow_right,
    feature_fading_baseline,
    diagonal_boost_coefficient,
    cluster_standardize_scale,
    cluster_standardize_offset,
    emitted_mapping_matrix,
):
    rows = tier_source_concatenated.shape[0]
    local_width = mapping_matrices_pile.shape[2]
    mixing_values_divided = local_width // CHANNELS_ONE_HEAD
    block = min(32, rows)
    blocks = rows // block
    full = lax.all_gather(tier_source_concatenated, "tp", axis=1, tiled=True)
    normed = layer_norm(
        full.astype(jnp.float32), tier_standardize_scale, tier_standardize_offset, 1e-05
    ).astype(jnp.bfloat16)
    first = jnp.cumsum(prompt_sizes_ordered) - prompt_sizes_ordered
    position = lax.axis_index("seq") * rows + jnp.arange(rows, dtype=jnp.int32)
    is_start = jnp.any(position[:, None] == first[None, :], axis=1)
    segment = jnp.sum((first[None, :] <= position[:, None]).astype(jnp.int32), axis=1)
    edge = from_behind(normed[rows - 1 :], "seq", 1)
    previous = jnp.concatenate([edge, normed[: rows - 1]], axis=0)
    previous = jnp.where(is_start[:, None], jnp.zeros_like(previous), previous)
    base = normed.astype(jnp.float32)
    delta = previous.astype(jnp.float32) - base
    shifted_blend = (base[None] + delta[None] * previous_item_mixers[:, None, :]).astype(
        jnp.bfloat16
    )
    projected = jnp.einsum(
        "itd,ide->ite", shifted_blend[:4], mapping_matrices_pile, preferred_element_type=jnp.float32
    )
    recept = projected[0].astype(jnp.bfloat16)
    key_rows = projected[1].astype(jnp.bfloat16)
    value_rows = projected[2].astype(jnp.bfloat16)
    gate = jax.nn.silu(projected[3]).astype(jnp.bfloat16)
    lowrank_decay_delta = jnp.tanh(
        jnp.dot(shifted_blend[4], fading_narrow_left, preferred_element_type=jnp.float32)
    ).astype(jnp.bfloat16)
    decay_logarithm = -feature_fading_baseline[None, :] * jnp.exp(
        jnp.dot(lowrank_decay_delta, fading_narrow_right, preferred_element_type=jnp.float32)
    )

    def split_heads(values):
        return (
            values.astype(jnp.float32)
            .reshape(blocks, block, mixing_values_divided, CHANNELS_ONE_HEAD)
            .transpose(0, 2, 1, 3)
        )

    inputs = (
        split_heads(recept),
        split_heads(key_rows),
        split_heads(value_rows),
        split_heads(decay_logarithm),
        segment.reshape(blocks, block),
        is_start.astype(jnp.float32).reshape(blocks, block),
    )
    order = jnp.arange(block)
    lower_incl = (order[None, :] <= order[:, None]).astype(jnp.float32)
    strictly = order[None, :] < order[:, None]
    diagonal_extra_contribution = diagonal_boost_coefficient.reshape(
        mixing_values_divided, CHANNELS_ONE_HEAD
    )

    def block_step(carry, item):
        running_recurrence_array, offset, alive = carry
        gating_rows_tile, query_array_tile, content_slab, lw_b, seg_b, start_b = item
        incl = jnp.einsum("ts,hsc->htc", lower_incl, lw_b, precision=highest)
        excl = incl - lw_b
        pair_ok = strictly & (seg_b[None, :] == seg_b[:, None])
        gap = jnp.minimum(excl[:, :, None, :] - incl[:, None, :, :], 0.0)
        weight = jnp.where(pair_ok[None, :, :, None], jnp.exp(gap), 0.0)
        scores = jnp.einsum(
            "htc,hsc,htsc->hts", gating_rows_tile, query_array_tile, weight, precision=highest
        )
        present_item_reward = jnp.sum(
            gating_rows_tile * diagonal_extra_contribution[:, None, :] * query_array_tile, axis=-1
        )
        seen = jnp.dot(lower_incl, start_b, precision=highest)
        valid = (seen == 0.0).astype(jnp.float32)
        carried = gating_rows_tile * jnp.exp(excl) * valid[None, :, None]
        level_ultimate_outcome = (
            jnp.einsum("hts,hsv->htv", scores, content_slab, precision=highest)
            + present_item_reward[..., None] * content_slab
        )
        level_ultimate_outcome = level_ultimate_outcome + jnp.einsum(
            "htc,hcv->htv", carried, running_recurrence_array, precision=highest
        )
        from_start = carried * alive * jnp.exp(offset)[:, None, :]
        total = incl[:, block - 1, :]
        keep = (seen[block - 1] == 0.0).astype(jnp.float32)
        tail_ok = (seg_b == seg_b[block - 1]).astype(jnp.float32)
        tail = query_array_tile * jnp.exp(total[:, None, :] - incl) * tail_ok[None, :, None]
        running_recurrence_array = keep * jnp.exp(total)[
            :, :, None
        ] * running_recurrence_array + jnp.einsum(
            "hsc,hsv->hcv", tail, content_slab, precision=highest
        )
        return (
            (running_recurrence_array, offset + total, alive * keep),
            (level_ultimate_outcome, from_start),
        )

    init = (
        jnp.zeros((mixing_values_divided, CHANNELS_ONE_HEAD, CHANNELS_ONE_HEAD), jnp.float32),
        jnp.zeros((mixing_values_divided, CHANNELS_ONE_HEAD), jnp.float32),
        jnp.float32(1.0),
    )
    (end_state, offset, alive), (outs, from_start) = lax.scan(block_step, init, inputs)
    decay_total = alive * jnp.exp(offset)

    devices = lax.axis_size("seq")
    packed = jnp.concatenate([end_state, decay_total[:, None, :]], axis=1)

    def combine(received, own):
        own_state, own_decay = own[:, :CHANNELS_ONE_HEAD], own[:, CHANNELS_ONE_HEAD:]
        got_state, got_decay = received[:, :CHANNELS_ONE_HEAD], received[:, CHANNELS_ONE_HEAD:]
        state = jnp.transpose(own_decay, (0, 2, 1)) * got_state + own_state
        return jnp.concatenate([state, own_decay * got_decay], axis=1)

    prefix = from_behind(packed, "seq", 1)
    distance = 1
    while distance < devices:
        prefix = combine(from_behind(prefix, "seq", distance), prefix)
        distance *= 2
    incoming = prefix[:, :CHANNELS_ONE_HEAD]
    outs = outs + jnp.einsum("bhtc,hcv->bhtv", from_start, incoming, precision=highest)
    wkv = outs.transpose(0, 2, 1, 3).reshape(rows, mixing_values_divided, CHANNELS_ONE_HEAD)
    mean = jnp.mean(wkv, axis=-1, keepdims=True)
    centred = wkv - mean
    spread = jnp.mean(centred * centred, axis=-1, keepdims=True)
    grouped = (centred * lax.rsqrt(spread + 0.00064)).reshape(
        rows, local_width
    ) * cluster_standardize_scale + cluster_standardize_offset
    gated = (grouped * gate.astype(jnp.float32)).astype(jnp.bfloat16)
    partial_sum = jnp.dot(gated, emitted_mapping_matrix, preferred_element_type=jnp.float32)
    summed = lax.psum(partial_sum.astype(jnp.bfloat16), "tp").astype(jnp.float32)
    mine = lax.dynamic_slice_in_dim(summed, lax.axis_index("tp") * local_width, local_width, 1)
    return (tier_source_concatenated.astype(jnp.float32) + mine).astype(jnp.bfloat16)


def solution(mesh):
    in_specs = (
        P("seq", "tp"),
        P(),
        P(),
        P(),
        P(),
        P(None, None, "tp"),
        P(),
        P(None, "tp"),
        P("tp"),
        P("tp"),
        P("tp"),
        P("tp"),
        P("tp", None),
    )
    out_specs = P("seq", "tp")
    return jax.shard_map(body, mesh=mesh, in_specs=in_specs, out_specs=out_specs, check_vma=False)
```

```python
import jax
import jax.numpy as jnp
from jax import lax
from jax.sharding import PartitionSpec as P

CHANNELS_ONE_HEAD = 64


highest = lax.Precision.HIGHEST


def from_behind(block, axis, distance):
    devices = range(lax.axis_size(axis))
    route = [(i - distance, i) for i in devices if i - distance in devices]
    return lax.ppermute(block, axis, route)


def layer_norm(rows, gain, bias, eps):
    mean = jnp.mean(rows, axis=-1, keepdims=True)
    centred = rows - mean
    spread = jnp.mean(centred * centred, axis=-1, keepdims=True)
    return centred * lax.rsqrt(spread + eps) * gain + bias


def body(
    tier_source_concatenated,
    prompt_sizes_ordered,
    tier_standardize_scale,
    tier_standardize_offset,
    previous_item_mixers,
    mapping_matrices_pile,
    fading_narrow_left,
    fading_narrow_right,
    feature_fading_baseline,
    diagonal_boost_coefficient,
    cluster_standardize_scale,
    cluster_standardize_offset,
    emitted_mapping_matrix,
):
    rows = tier_source_concatenated.shape[0]
    local_width = mapping_matrices_pile.shape[2]
    mixing_values_divided = local_width // CHANNELS_ONE_HEAD
    block = min(32, rows)
    blocks = rows // block
    full = lax.all_gather(tier_source_concatenated, "tp", axis=1, tiled=True)
    normed = layer_norm(
        full.astype(jnp.float32), tier_standardize_scale, tier_standardize_offset, 1e-05
    ).astype(jnp.bfloat16)
    first = jnp.cumsum(prompt_sizes_ordered) - prompt_sizes_ordered
    position = lax.axis_index("seq") * rows + jnp.arange(rows, dtype=jnp.int32)
    is_start = jnp.any(position[:, None] == first[None, :], axis=1)
    segment = jnp.sum((first[None, :] <= position[:, None]).astype(jnp.int32), axis=1)
    edge = from_behind(normed[rows - 1 :], "seq", 1)
    previous = jnp.concatenate([edge, normed[: rows - 1]], axis=0)
    previous = jnp.where(is_start[:, None], jnp.zeros_like(previous), previous)
    base = normed.astype(jnp.float32)
    delta = previous.astype(jnp.float32) - base
    shifted_blend = (base[None] + delta[None] * previous_item_mixers[:, None, :]).astype(
        jnp.bfloat16
    )
    projected = jnp.einsum(
        "itd,ide->ite", shifted_blend[:4], mapping_matrices_pile, preferred_element_type=jnp.float32
    )
    recept = projected[0].astype(jnp.bfloat16)
    key_rows = projected[1].astype(jnp.bfloat16)
    value_rows = projected[2].astype(jnp.bfloat16)
    gate = jax.nn.silu(projected[3]).astype(jnp.bfloat16)
    lowrank_decay_delta = jnp.tanh(
        jnp.dot(shifted_blend[4], fading_narrow_left, preferred_element_type=jnp.float32)
    ).astype(jnp.bfloat16)
    decay_logarithm = -feature_fading_baseline[None, :] * jnp.exp(
        jnp.dot(lowrank_decay_delta, fading_narrow_right, preferred_element_type=jnp.float32)
    )

    def split_heads(values):
        return (
            values.astype(jnp.float32)
            .reshape(blocks, block, mixing_values_divided, CHANNELS_ONE_HEAD)
            .transpose(0, 2, 1, 3)
        )

    inputs = (
        split_heads(recept),
        split_heads(key_rows),
        split_heads(value_rows),
        split_heads(decay_logarithm),
        segment.reshape(blocks, block),
        is_start.astype(jnp.float32).reshape(blocks, block),
    )
    order = jnp.arange(block)
    lower_incl = (order[None, :] <= order[:, None]).astype(jnp.float32)
    strictly = order[None, :] < order[:, None]
    diagonal_extra_contribution = diagonal_boost_coefficient.reshape(
        mixing_values_divided, CHANNELS_ONE_HEAD
    )

    def block_step(carry, item):
        running_recurrence_array, offset, alive = carry
        gating_rows_tile, query_array_tile, content_slab, lw_b, seg_b, start_b = item
        incl = jnp.einsum("ts,hsc->htc", lower_incl, lw_b, precision=highest)
        excl = incl - lw_b
        pair_ok = strictly & (seg_b[None, :] == seg_b[:, None])
        gap = jnp.minimum(excl[:, :, None, :] - incl[:, None, :, :], 0.0)
        weight = jnp.where(pair_ok[None, :, :, None], jnp.exp(gap), 0.0)
        scores = jnp.einsum(
            "htc,hsc,htsc->hts", gating_rows_tile, query_array_tile, weight, precision=highest
        )
        present_item_reward = jnp.sum(
            gating_rows_tile * diagonal_extra_contribution[:, None, :] * query_array_tile, axis=-1
        )
        seen = jnp.dot(lower_incl, start_b, precision=highest)
        valid = (seen == 0.0).astype(jnp.float32)
        carried = gating_rows_tile * jnp.exp(excl) * valid[None, :, None]
        level_ultimate_outcome = (
            jnp.einsum("hts,hsv->htv", scores, content_slab, precision=highest)
            + present_item_reward[..., None] * content_slab
        )
        level_ultimate_outcome = level_ultimate_outcome + jnp.einsum(
            "htc,hcv->htv", carried, running_recurrence_array, precision=highest
        )
        from_start = carried * alive * jnp.exp(offset)[:, None, :]
        total = incl[:, block - 1, :]
        keep = (seen[block - 1] == 0.0).astype(jnp.float32)
        tail_ok = (seg_b == seg_b[block - 1]).astype(jnp.float32)
        tail = query_array_tile * jnp.exp(total[:, None, :] - incl) * tail_ok[None, :, None]
        running_recurrence_array = keep * jnp.exp(total)[
            :, :, None
        ] * running_recurrence_array + jnp.einsum(
            "hsc,hsv->hcv", tail, content_slab, precision=highest
        )
        return (
            (running_recurrence_array, offset + total, alive * keep),
            (level_ultimate_outcome, from_start),
        )

    init = (
        jnp.zeros((mixing_values_divided, CHANNELS_ONE_HEAD, CHANNELS_ONE_HEAD), jnp.float32),
        jnp.zeros((mixing_values_divided, CHANNELS_ONE_HEAD), jnp.float32),
        jnp.float32(1.0),
    )
    decay_heads = decay_logarithm.reshape(rows, mixing_values_divided, CHANNELS_ONE_HEAD).transpose(1, 0, 2)
    suffix_incl = jnp.flip(jnp.cumsum(jnp.flip(decay_heads, 1), axis=1), 1)
    suffix_excl = jnp.concatenate([suffix_incl[:, 1:], jnp.zeros_like(suffix_incl[:, :1])], axis=1)
    in_tail = (segment == segment[rows - 1]).astype(jnp.float32)
    key_heads = key_rows.astype(jnp.float32).reshape(rows, mixing_values_divided, CHANNELS_ONE_HEAD)
    value_heads = value_rows.astype(jnp.float32).reshape(rows, mixing_values_divided, CHANNELS_ONE_HEAD)
    tail_keys = key_heads.transpose(1, 0, 2) * jnp.exp(suffix_excl) * in_tail[None, :, None]
    end_state = jnp.einsum("hsc,shv->hcv", tail_keys, value_heads, precision=highest)
    decay_total = jnp.all(jnp.logical_not(is_start)).astype(jnp.float32) * jnp.exp(suffix_incl[:, 0])
    carry = init
    outs, from_start = [], []
    for index in range(blocks):
        carry, (block_out, block_from_start) = block_step(carry, tuple(part[index] for part in inputs))
        outs.append(block_out)
        from_start.append(block_from_start)
    outs = jnp.stack(outs)
    from_start = jnp.stack(from_start)

    devices = lax.axis_size("seq")
    packed = jnp.concatenate([end_state, decay_total[:, None, :]], axis=1)

    def combine(received, own):
        own_state, own_decay = own[:, :CHANNELS_ONE_HEAD], own[:, CHANNELS_ONE_HEAD:]
        got_state, got_decay = received[:, :CHANNELS_ONE_HEAD], received[:, CHANNELS_ONE_HEAD:]
        state = jnp.transpose(own_decay, (0, 2, 1)) * got_state + own_state
        return jnp.concatenate([state, own_decay * got_decay], axis=1)

    prefix = from_behind(packed, "seq", 1)
    distance = 1
    while distance < devices:
        prefix = combine(from_behind(prefix, "seq", distance), prefix)
        distance *= 2
    incoming = prefix[:, :CHANNELS_ONE_HEAD]
    outs = outs + jnp.einsum("bhtc,hcv->bhtv", from_start, incoming, precision=highest)
    wkv = outs.transpose(0, 2, 1, 3).reshape(rows, mixing_values_divided, CHANNELS_ONE_HEAD)
    mean = jnp.mean(wkv, axis=-1, keepdims=True)
    centred = wkv - mean
    spread = jnp.mean(centred * centred, axis=-1, keepdims=True)
    grouped = (centred * lax.rsqrt(spread + 0.00064)).reshape(
        rows, local_width
    ) * cluster_standardize_scale + cluster_standardize_offset
    gated = (grouped * gate.astype(jnp.float32)).astype(jnp.bfloat16)
    partial_sum = jnp.dot(gated, emitted_mapping_matrix, preferred_element_type=jnp.float32)
    parts = lax.axis_size("tp")
    pieces = partial_sum.astype(jnp.bfloat16).reshape(rows, parts, local_width).transpose(1, 0, 2)
    pieces = lax.all_to_all(pieces, "tp", 0, 0, tiled=True)
    mine = jnp.sum(pieces.astype(jnp.float32), axis=0)
    return (tier_source_concatenated.astype(jnp.float32) + mine).astype(jnp.bfloat16)


def solution(mesh):
    in_specs = (
        P("seq", "tp"),
        P(),
        P(),
        P(),
        P(),
        P(None, None, "tp"),
        P(),
        P(None, "tp"),
        P("tp"),
        P("tp"),
        P("tp"),
        P("tp"),
        P("tp", None),
    )
    out_specs = P("seq", "tp")
    return jax.shard_map(body, mesh=mesh, in_specs=in_specs, out_specs=out_specs, check_vma=False)
```

```python
import math

import jax
import jax.numpy as jnp
from jax import lax
from jax.sharding import PartitionSpec as P

CHANNELS_ONE_HEAD = 64


highest = lax.Precision.HIGHEST


SEQ = ("seq_hi", "seq_lo")


def size_of(axes):
    return math.prod(lax.axis_size(axis) for axis in axes)


def from_behind(block, axis, distance):
    devices = range(size_of(axis))
    route = [(i - distance, i) for i in devices if i - distance in devices]
    return lax.ppermute(block, axis, route)


def layer_norm(rows, gain, bias, eps):
    mean = jnp.mean(rows, axis=-1, keepdims=True)
    centred = rows - mean
    spread = jnp.mean(centred * centred, axis=-1, keepdims=True)
    return centred * lax.rsqrt(spread + eps) * gain + bias


def body(
    tier_source_concatenated,
    prompt_sizes_ordered,
    tier_standardize_scale,
    tier_standardize_offset,
    previous_item_mixers,
    mapping_matrices_pile,
    fading_narrow_left,
    fading_narrow_right,
    feature_fading_baseline,
    diagonal_boost_coefficient,
    cluster_standardize_scale,
    cluster_standardize_offset,
    emitted_mapping_matrix,
):
    rows = tier_source_concatenated.shape[0]
    local_width = mapping_matrices_pile.shape[2]
    mixing_values_divided = local_width // CHANNELS_ONE_HEAD
    block = min(32, rows)
    blocks = rows // block
    full = lax.all_gather(tier_source_concatenated, "tp", axis=1, tiled=True)
    normed = layer_norm(
        full.astype(jnp.float32), tier_standardize_scale, tier_standardize_offset, 1e-05
    ).astype(jnp.bfloat16)
    first = jnp.cumsum(prompt_sizes_ordered) - prompt_sizes_ordered
    position = lax.axis_index(SEQ) * rows + jnp.arange(rows, dtype=jnp.int32)
    is_start = jnp.any(position[:, None] == first[None, :], axis=1)
    segment = jnp.sum((first[None, :] <= position[:, None]).astype(jnp.int32), axis=1)
    edge = from_behind(normed[rows - 1 :], SEQ, 1)
    previous = jnp.concatenate([edge, normed[: rows - 1]], axis=0)
    previous = jnp.where(is_start[:, None], jnp.zeros_like(previous), previous)
    base = normed.astype(jnp.float32)
    delta = previous.astype(jnp.float32) - base
    shifted_blend = (base[None] + delta[None] * previous_item_mixers[:, None, :]).astype(
        jnp.bfloat16
    )
    projected = jnp.einsum(
        "itd,ide->ite", shifted_blend[:4], mapping_matrices_pile, preferred_element_type=jnp.float32
    )
    recept = projected[0].astype(jnp.bfloat16)
    key_rows = projected[1].astype(jnp.bfloat16)
    value_rows = projected[2].astype(jnp.bfloat16)
    gate = jax.nn.silu(projected[3]).astype(jnp.bfloat16)
    lowrank_decay_delta = jnp.tanh(
        jnp.dot(shifted_blend[4], fading_narrow_left, preferred_element_type=jnp.float32)
    ).astype(jnp.bfloat16)
    decay_logarithm = -feature_fading_baseline[None, :] * jnp.exp(
        jnp.dot(lowrank_decay_delta, fading_narrow_right, preferred_element_type=jnp.float32)
    )

    def split_heads(values):
        return (
            values.astype(jnp.float32)
            .reshape(blocks, block, mixing_values_divided, CHANNELS_ONE_HEAD)
            .transpose(0, 2, 1, 3)
        )

    inputs = (
        split_heads(recept),
        split_heads(key_rows),
        split_heads(value_rows),
        split_heads(decay_logarithm),
        segment.reshape(blocks, block),
        is_start.astype(jnp.float32).reshape(blocks, block),
    )
    order = jnp.arange(block)
    lower_incl = (order[None, :] <= order[:, None]).astype(jnp.float32)
    strictly = order[None, :] < order[:, None]
    diagonal_extra_contribution = diagonal_boost_coefficient.reshape(
        mixing_values_divided, CHANNELS_ONE_HEAD
    )

    def block_step(carry, item):
        running_recurrence_array, offset, alive = carry
        gating_rows_tile, query_array_tile, content_slab, lw_b, seg_b, start_b = item
        incl = jnp.einsum("ts,hsc->htc", lower_incl, lw_b, precision=highest)
        excl = incl - lw_b
        pair_ok = strictly & (seg_b[None, :] == seg_b[:, None])
        gap = jnp.minimum(excl[:, :, None, :] - incl[:, None, :, :], 0.0)
        weight = jnp.where(pair_ok[None, :, :, None], jnp.exp(gap), 0.0)
        scores = jnp.einsum(
            "htc,hsc,htsc->hts", gating_rows_tile, query_array_tile, weight, precision=highest
        )
        present_item_reward = jnp.sum(
            gating_rows_tile * diagonal_extra_contribution[:, None, :] * query_array_tile, axis=-1
        )
        seen = jnp.dot(lower_incl, start_b, precision=highest)
        valid = (seen == 0.0).astype(jnp.float32)
        carried = gating_rows_tile * jnp.exp(excl) * valid[None, :, None]
        level_ultimate_outcome = (
            jnp.einsum("hts,hsv->htv", scores, content_slab, precision=highest)
            + present_item_reward[..., None] * content_slab
        )
        level_ultimate_outcome = level_ultimate_outcome + jnp.einsum(
            "htc,hcv->htv", carried, running_recurrence_array, precision=highest
        )
        from_start = carried * alive * jnp.exp(offset)[:, None, :]
        total = incl[:, block - 1, :]
        keep = (seen[block - 1] == 0.0).astype(jnp.float32)
        tail_ok = (seg_b == seg_b[block - 1]).astype(jnp.float32)
        tail = query_array_tile * jnp.exp(total[:, None, :] - incl) * tail_ok[None, :, None]
        running_recurrence_array = keep * jnp.exp(total)[
            :, :, None
        ] * running_recurrence_array + jnp.einsum(
            "hsc,hsv->hcv", tail, content_slab, precision=highest
        )
        return (
            (running_recurrence_array, offset + total, alive * keep),
            (level_ultimate_outcome, from_start),
        )

    init = (
        jnp.zeros((mixing_values_divided, CHANNELS_ONE_HEAD, CHANNELS_ONE_HEAD), jnp.float32),
        jnp.zeros((mixing_values_divided, CHANNELS_ONE_HEAD), jnp.float32),
        jnp.float32(1.0),
    )
    decay_heads = decay_logarithm.reshape(rows, mixing_values_divided, CHANNELS_ONE_HEAD).transpose(1, 0, 2)
    suffix_incl = jnp.flip(jnp.cumsum(jnp.flip(decay_heads, 1), axis=1), 1)
    suffix_excl = jnp.concatenate([suffix_incl[:, 1:], jnp.zeros_like(suffix_incl[:, :1])], axis=1)
    in_tail = (segment == segment[rows - 1]).astype(jnp.float32)
    key_heads = key_rows.astype(jnp.float32).reshape(rows, mixing_values_divided, CHANNELS_ONE_HEAD)
    value_heads = value_rows.astype(jnp.float32).reshape(rows, mixing_values_divided, CHANNELS_ONE_HEAD)
    tail_keys = key_heads.transpose(1, 0, 2) * jnp.exp(suffix_excl) * in_tail[None, :, None]
    end_state = jnp.einsum("hsc,shv->hcv", tail_keys, value_heads, precision=highest)
    decay_total = jnp.all(jnp.logical_not(is_start)).astype(jnp.float32) * jnp.exp(suffix_incl[:, 0])
    _, (outs, from_start) = lax.scan(block_step, init, inputs)

    packed = jnp.concatenate([end_state, decay_total[:, None, :]], axis=1)

    def fold(gathered, count):
        state = jnp.zeros_like(end_state)
        decay = jnp.ones_like(decay_total)
        for index in range(gathered.shape[0]):
            take = index < count
            piece = gathered[index]
            state = jnp.where(take, piece[:, CHANNELS_ONE_HEAD, :, None] * state + piece[:, :CHANNELS_ONE_HEAD], state)
            decay = jnp.where(take, piece[:, CHANNELS_ONE_HEAD] * decay, decay)
        return state, decay

    low = lax.axis_index("seq_lo")
    neighbours = lax.all_gather(packed, "seq_lo")
    inner_state, inner_decay = fold(neighbours, low)
    group_state, group_decay = fold(neighbours, lax.axis_size("seq_lo"))
    group = jnp.concatenate([group_state, group_decay[:, None, :]], axis=1)
    entering, _ = fold(lax.all_gather(group, "seq_hi"), lax.axis_index("seq_hi"))
    incoming = inner_decay[:, :, None] * entering + inner_state
    outs = outs + jnp.einsum("bhtc,hcv->bhtv", from_start, incoming, precision=highest)
    wkv = outs.transpose(0, 2, 1, 3).reshape(rows, mixing_values_divided, CHANNELS_ONE_HEAD)
    mean = jnp.mean(wkv, axis=-1, keepdims=True)
    centred = wkv - mean
    spread = jnp.mean(centred * centred, axis=-1, keepdims=True)
    grouped = (centred * lax.rsqrt(spread + 0.00064)).reshape(
        rows, local_width
    ) * cluster_standardize_scale + cluster_standardize_offset
    gated = (grouped * gate.astype(jnp.float32)).astype(jnp.bfloat16)
    partial_sum = jnp.dot(gated, emitted_mapping_matrix, preferred_element_type=jnp.float32)
    parts = lax.axis_size("tp")
    pieces = partial_sum.astype(jnp.bfloat16).reshape(rows, parts, local_width).transpose(1, 0, 2)
    pieces = lax.all_to_all(pieces, "tp", 0, 0, tiled=True)
    mine = jnp.sum(pieces.astype(jnp.float32), axis=0)
    return (tier_source_concatenated.astype(jnp.float32) + mine).astype(jnp.bfloat16)


def solution(mesh):
    groups = 8 if mesh.shape["seq"] % 8 == 0 else 1
    devices = mesh.devices.reshape(mesh.shape["seq"] // groups, groups, mesh.shape["tp"])
    mesh = jax.sharding.Mesh(devices, ("seq_hi", "seq_lo", "tp"))
    in_specs = (
        P(SEQ, "tp"),
        P(),
        P(),
        P(),
        P(),
        P(None, None, "tp"),
        P(),
        P(None, "tp"),
        P("tp"),
        P("tp"),
        P("tp"),
        P("tp"),
        P("tp", None),
    )
    out_specs = P(SEQ, "tp")
    return jax.shard_map(body, mesh=mesh, in_specs=in_specs, out_specs=out_specs, check_vma=False)
```

```python
import math

import jax
import jax.numpy as jnp
from jax import lax
from jax.sharding import PartitionSpec as P

CHANNELS_ONE_HEAD = 64


highest = lax.Precision.HIGHEST


SEQ = ("seq_hi", "seq_lo")


def gather(block, axis):
    copies = jnp.broadcast_to(block[None], (lax.axis_size(axis),) + block.shape)
    return lax.all_to_all(copies, axis, 0, 0, tiled=True)


def size_of(axes):
    return math.prod(lax.axis_size(axis) for axis in axes)


def from_behind(block, axis, distance):
    devices = range(size_of(axis))
    route = [(i - distance, i) for i in devices if i - distance in devices]
    return lax.ppermute(block, axis, route)


def layer_norm(rows, gain, bias, eps):
    mean = jnp.mean(rows, axis=-1, keepdims=True)
    centred = rows - mean
    spread = jnp.mean(centred * centred, axis=-1, keepdims=True)
    return centred * lax.rsqrt(spread + eps) * gain + bias


def body(
    tier_source_concatenated,
    prompt_sizes_ordered,
    tier_standardize_scale,
    tier_standardize_offset,
    previous_item_mixers,
    mapping_matrices_pile,
    fading_narrow_left,
    fading_narrow_right,
    feature_fading_baseline,
    diagonal_boost_coefficient,
    cluster_standardize_scale,
    cluster_standardize_offset,
    emitted_mapping_matrix,
):
    rows = tier_source_concatenated.shape[0]
    local_width = mapping_matrices_pile.shape[2]
    mixing_values_divided = local_width // CHANNELS_ONE_HEAD
    block = min(32, rows)
    blocks = rows // block
    full = lax.all_gather(tier_source_concatenated, "tp", axis=1, tiled=True)
    normed = layer_norm(
        full.astype(jnp.float32), tier_standardize_scale, tier_standardize_offset, 1e-05
    ).astype(jnp.bfloat16)
    first = jnp.cumsum(prompt_sizes_ordered) - prompt_sizes_ordered
    position = lax.axis_index(SEQ) * rows + jnp.arange(rows, dtype=jnp.int32)
    is_start = jnp.any(position[:, None] == first[None, :], axis=1)
    segment = jnp.sum((first[None, :] <= position[:, None]).astype(jnp.int32), axis=1)
    edge = from_behind(normed[rows - 1 :], SEQ, 1)
    previous = jnp.concatenate([edge, normed[: rows - 1]], axis=0)
    previous = jnp.where(is_start[:, None], jnp.zeros_like(previous), previous)
    base = normed.astype(jnp.float32)
    delta = previous.astype(jnp.float32) - base
    shifted_blend = (base[None] + delta[None] * previous_item_mixers[:, None, :]).astype(
        jnp.bfloat16
    )
    projected = jnp.einsum(
        "itd,ide->ite", shifted_blend[:4], mapping_matrices_pile, preferred_element_type=jnp.float32
    )
    recept = projected[0].astype(jnp.bfloat16)
    key_rows = projected[1].astype(jnp.bfloat16)
    value_rows = projected[2].astype(jnp.bfloat16)
    gate = jax.nn.silu(projected[3]).astype(jnp.bfloat16)
    lowrank_decay_delta = jnp.tanh(
        jnp.dot(shifted_blend[4], fading_narrow_left, preferred_element_type=jnp.float32)
    ).astype(jnp.bfloat16)
    decay_logarithm = -feature_fading_baseline[None, :] * jnp.exp(
        jnp.dot(lowrank_decay_delta, fading_narrow_right, preferred_element_type=jnp.float32)
    )

    def split_heads(values):
        return (
            values.astype(jnp.float32)
            .reshape(blocks, block, mixing_values_divided, CHANNELS_ONE_HEAD)
            .transpose(0, 2, 1, 3)
        )

    inputs = (
        split_heads(recept),
        split_heads(key_rows),
        split_heads(value_rows),
        split_heads(decay_logarithm),
        segment.reshape(blocks, block),
        is_start.astype(jnp.float32).reshape(blocks, block),
    )
    order = jnp.arange(block)
    lower_incl = (order[None, :] <= order[:, None]).astype(jnp.float32)
    strictly = order[None, :] < order[:, None]
    diagonal_extra_contribution = diagonal_boost_coefficient.reshape(
        mixing_values_divided, CHANNELS_ONE_HEAD
    )

    def block_step(carry, item):
        running_recurrence_array, offset, alive = carry
        gating_rows_tile, query_array_tile, content_slab, lw_b, seg_b, start_b = item
        incl = jnp.einsum("ts,hsc->htc", lower_incl, lw_b, precision=highest)
        excl = incl - lw_b
        pair_ok = strictly & (seg_b[None, :] == seg_b[:, None])
        gap = jnp.minimum(excl[:, :, None, :] - incl[:, None, :, :], 0.0)
        weight = jnp.where(pair_ok[None, :, :, None], jnp.exp(gap), 0.0)
        scores = jnp.einsum(
            "htc,hsc,htsc->hts", gating_rows_tile, query_array_tile, weight, precision=highest
        )
        present_item_reward = jnp.sum(
            gating_rows_tile * diagonal_extra_contribution[:, None, :] * query_array_tile, axis=-1
        )
        seen = jnp.dot(lower_incl, start_b, precision=highest)
        valid = (seen == 0.0).astype(jnp.float32)
        carried = gating_rows_tile * jnp.exp(excl) * valid[None, :, None]
        level_ultimate_outcome = (
            jnp.einsum("hts,hsv->htv", scores, content_slab, precision=highest)
            + present_item_reward[..., None] * content_slab
        )
        level_ultimate_outcome = level_ultimate_outcome + jnp.einsum(
            "htc,hcv->htv", carried, running_recurrence_array, precision=highest
        )
        from_start = carried * alive * jnp.exp(offset)[:, None, :]
        total = incl[:, block - 1, :]
        keep = (seen[block - 1] == 0.0).astype(jnp.float32)
        tail_ok = (seg_b == seg_b[block - 1]).astype(jnp.float32)
        tail = query_array_tile * jnp.exp(total[:, None, :] - incl) * tail_ok[None, :, None]
        running_recurrence_array = keep * jnp.exp(total)[
            :, :, None
        ] * running_recurrence_array + jnp.einsum(
            "hsc,hsv->hcv", tail, content_slab, precision=highest
        )
        return (
            (running_recurrence_array, offset + total, alive * keep),
            (level_ultimate_outcome, from_start),
        )

    init = (
        jnp.zeros((mixing_values_divided, CHANNELS_ONE_HEAD, CHANNELS_ONE_HEAD), jnp.float32),
        jnp.zeros((mixing_values_divided, CHANNELS_ONE_HEAD), jnp.float32),
        jnp.float32(1.0),
    )
    decay_heads = decay_logarithm.reshape(rows, mixing_values_divided, CHANNELS_ONE_HEAD).transpose(1, 0, 2)
    later = (jnp.arange(rows)[None, :] > jnp.arange(rows)[:, None]).astype(jnp.float32)
    suffix_excl = jnp.einsum("sj,hjc->hsc", later, decay_heads, precision=highest)
    decay_sum = jnp.sum(decay_heads, axis=1)
    in_tail = (segment == segment[rows - 1]).astype(jnp.float32)
    key_heads = key_rows.astype(jnp.float32).reshape(rows, mixing_values_divided, CHANNELS_ONE_HEAD)
    value_heads = value_rows.astype(jnp.float32).reshape(rows, mixing_values_divided, CHANNELS_ONE_HEAD)
    tail_keys = key_heads.transpose(1, 0, 2) * jnp.exp(suffix_excl) * in_tail[None, :, None]
    end_state = jnp.einsum("hsc,shv->hcv", tail_keys, value_heads, precision=highest)
    decay_total = jnp.all(jnp.logical_not(is_start)).astype(jnp.float32) * jnp.exp(decay_sum)
    _, (outs, from_start) = lax.scan(block_step, init, inputs)

    packed = jnp.concatenate([end_state, decay_total[:, None, :]], axis=1)

    def fold(gathered, count):
        state = jnp.zeros_like(end_state)
        decay = jnp.ones_like(decay_total)
        for index in range(gathered.shape[0]):
            take = index < count
            piece = gathered[index]
            state = jnp.where(take, piece[:, CHANNELS_ONE_HEAD, :, None] * state + piece[:, :CHANNELS_ONE_HEAD], state)
            decay = jnp.where(take, piece[:, CHANNELS_ONE_HEAD] * decay, decay)
        return state, decay

    low = lax.axis_index("seq_lo")
    neighbours = gather(packed, "seq_lo")
    inner_state, inner_decay = fold(neighbours, low)
    group_state, group_decay = fold(neighbours, lax.axis_size("seq_lo"))
    group = jnp.concatenate([group_state, group_decay[:, None, :]], axis=1)
    entering, _ = fold(gather(group, "seq_hi"), lax.axis_index("seq_hi"))
    incoming = inner_decay[:, :, None] * entering + inner_state
    outs = outs + jnp.einsum("bhtc,hcv->bhtv", from_start, incoming, precision=highest)
    wkv = outs.transpose(0, 2, 1, 3).reshape(rows, mixing_values_divided, CHANNELS_ONE_HEAD)
    mean = jnp.mean(wkv, axis=-1, keepdims=True)
    centred = wkv - mean
    spread = jnp.mean(centred * centred, axis=-1, keepdims=True)
    grouped = (centred * lax.rsqrt(spread + 0.00064)).reshape(
        rows, local_width
    ) * cluster_standardize_scale + cluster_standardize_offset
    gated = (grouped * gate.astype(jnp.float32)).astype(jnp.bfloat16)
    partial_sum = jnp.dot(gated, emitted_mapping_matrix, preferred_element_type=jnp.float32)
    parts = lax.axis_size("tp")
    pieces = partial_sum.astype(jnp.bfloat16).reshape(rows, parts, local_width).transpose(1, 0, 2)
    pieces = lax.all_to_all(pieces, "tp", 0, 0, tiled=True)
    mine = jnp.sum(pieces.astype(jnp.float32), axis=0)
    return (tier_source_concatenated.astype(jnp.float32) + mine).astype(jnp.bfloat16)


def solution(mesh):
    groups = 8 if mesh.shape["seq"] % 8 == 0 else 1
    devices = mesh.devices.reshape(mesh.shape["seq"] // groups, groups, mesh.shape["tp"])
    mesh = jax.sharding.Mesh(devices, ("seq_hi", "seq_lo", "tp"))
    in_specs = (
        P(SEQ, "tp"),
        P(),
        P(),
        P(),
        P(),
        P(None, None, "tp"),
        P(),
        P(None, "tp"),
        P("tp"),
        P("tp"),
        P("tp"),
        P("tp"),
        P("tp", None),
    )
    out_specs = P(SEQ, "tp")
    return jax.shard_map(body, mesh=mesh, in_specs=in_specs, out_specs=out_specs, check_vma=False)
```

```python
import math

import jax
import jax.numpy as jnp
from jax import lax
from jax.sharding import PartitionSpec as P

CHANNELS_ONE_HEAD = 64


highest = lax.Precision.HIGHEST


SEQ = ("seq_hi", "seq_lo")


def size_of(axes):
    return math.prod(lax.axis_size(axis) for axis in axes)


def from_behind(block, axis, distance):
    devices = range(size_of(axis))
    route = [(i - distance, i) for i in devices if i - distance in devices]
    return lax.ppermute(block, axis, route)


def layer_norm(rows, gain, bias, eps):
    mean = jnp.mean(rows, axis=-1, keepdims=True)
    centred = rows - mean
    spread = jnp.mean(centred * centred, axis=-1, keepdims=True)
    return centred * lax.rsqrt(spread + eps) * gain + bias


def body(
    tier_source_concatenated,
    prompt_sizes_ordered,
    tier_standardize_scale,
    tier_standardize_offset,
    previous_item_mixers,
    mapping_matrices_pile,
    fading_narrow_left,
    fading_narrow_right,
    feature_fading_baseline,
    diagonal_boost_coefficient,
    cluster_standardize_scale,
    cluster_standardize_offset,
    emitted_mapping_matrix,
):
    rows = tier_source_concatenated.shape[0]
    local_width = mapping_matrices_pile.shape[2]
    mixing_values_divided = local_width // CHANNELS_ONE_HEAD
    block = min(32, rows)
    blocks = rows // block
    full = lax.all_gather(tier_source_concatenated, "tp", axis=1, tiled=True)
    normed = layer_norm(
        full.astype(jnp.float32), tier_standardize_scale, tier_standardize_offset, 1e-05
    ).astype(jnp.bfloat16)
    first = jnp.cumsum(prompt_sizes_ordered) - prompt_sizes_ordered
    position = lax.axis_index(SEQ) * rows + jnp.arange(rows, dtype=jnp.int32)
    is_start = jnp.any(position[:, None] == first[None, :], axis=1)
    segment = jnp.sum((first[None, :] <= position[:, None]).astype(jnp.int32), axis=1)
    edge = from_behind(normed[rows - 1 :], SEQ, 1)
    previous = jnp.concatenate([edge, normed[: rows - 1]], axis=0)
    previous = jnp.where(is_start[:, None], jnp.zeros_like(previous), previous)
    base = normed.astype(jnp.float32)
    delta = previous.astype(jnp.float32) - base
    shifted_blend = (base[None] + delta[None] * previous_item_mixers[:, None, :]).astype(
        jnp.bfloat16
    )
    projected = jnp.einsum(
        "itd,ide->ite", shifted_blend[:4], mapping_matrices_pile, preferred_element_type=jnp.float32
    )
    recept = projected[0].astype(jnp.bfloat16)
    key_rows = projected[1].astype(jnp.bfloat16)
    value_rows = projected[2].astype(jnp.bfloat16)
    gate = jax.nn.silu(projected[3]).astype(jnp.bfloat16)
    lowrank_decay_delta = jnp.tanh(
        jnp.dot(shifted_blend[4], fading_narrow_left, preferred_element_type=jnp.float32)
    ).astype(jnp.bfloat16)
    decay_logarithm = -feature_fading_baseline[None, :] * jnp.exp(
        jnp.dot(lowrank_decay_delta, fading_narrow_right, preferred_element_type=jnp.float32)
    )

    def split_heads(values):
        return (
            values.astype(jnp.float32)
            .reshape(blocks, block, mixing_values_divided, CHANNELS_ONE_HEAD)
            .transpose(0, 2, 1, 3)
        )

    inputs = (
        split_heads(recept),
        split_heads(key_rows),
        split_heads(value_rows),
        split_heads(decay_logarithm),
        segment.reshape(blocks, block),
        is_start.astype(jnp.float32).reshape(blocks, block),
    )
    order = jnp.arange(block)
    lower_incl = (order[None, :] <= order[:, None]).astype(jnp.float32)
    strictly = order[None, :] < order[:, None]
    diagonal_extra_contribution = diagonal_boost_coefficient.reshape(
        mixing_values_divided, CHANNELS_ONE_HEAD
    )

    def block_step(carry, item):
        running_recurrence_array, offset, alive = carry
        gating_rows_tile, query_array_tile, content_slab, lw_b, seg_b, start_b = item
        incl = jnp.einsum("ts,hsc->htc", lower_incl, lw_b, precision=highest)
        excl = incl - lw_b
        pair_ok = strictly & (seg_b[None, :] == seg_b[:, None])
        gap = jnp.minimum(excl[:, :, None, :] - incl[:, None, :, :], 0.0)
        weight = jnp.where(pair_ok[None, :, :, None], jnp.exp(gap), 0.0)
        scores = jnp.einsum(
            "htc,hsc,htsc->hts", gating_rows_tile, query_array_tile, weight, precision=highest
        )
        present_item_reward = jnp.sum(
            gating_rows_tile * diagonal_extra_contribution[:, None, :] * query_array_tile, axis=-1
        )
        seen = jnp.dot(lower_incl, start_b, precision=highest)
        valid = (seen == 0.0).astype(jnp.float32)
        carried = gating_rows_tile * jnp.exp(excl) * valid[None, :, None]
        level_ultimate_outcome = (
            jnp.einsum("hts,hsv->htv", scores, content_slab, precision=highest)
            + present_item_reward[..., None] * content_slab
        )
        level_ultimate_outcome = level_ultimate_outcome + jnp.einsum(
            "htc,hcv->htv", carried, running_recurrence_array, precision=highest
        )
        from_start = carried * alive * jnp.exp(offset)[:, None, :]
        total = incl[:, block - 1, :]
        keep = (seen[block - 1] == 0.0).astype(jnp.float32)
        tail_ok = (seg_b == seg_b[block - 1]).astype(jnp.float32)
        tail = query_array_tile * jnp.exp(total[:, None, :] - incl) * tail_ok[None, :, None]
        running_recurrence_array = keep * jnp.exp(total)[
            :, :, None
        ] * running_recurrence_array + jnp.einsum(
            "hsc,hsv->hcv", tail, content_slab, precision=highest
        )
        return (
            (running_recurrence_array, offset + total, alive * keep),
            (level_ultimate_outcome, from_start),
        )

    init = (
        jnp.zeros((mixing_values_divided, CHANNELS_ONE_HEAD, CHANNELS_ONE_HEAD), jnp.float32),
        jnp.zeros((mixing_values_divided, CHANNELS_ONE_HEAD), jnp.float32),
        jnp.float32(1.0),
    )
    decay_heads = decay_logarithm.reshape(rows, mixing_values_divided, CHANNELS_ONE_HEAD).transpose(1, 0, 2)
    later = (jnp.arange(rows)[None, :] > jnp.arange(rows)[:, None]).astype(jnp.float32)
    suffix_excl = jnp.einsum("sj,hjc->hsc", later, decay_heads, precision=highest)
    decay_sum = jnp.sum(decay_heads, axis=1)
    in_tail = (segment == segment[rows - 1]).astype(jnp.float32)
    key_heads = key_rows.astype(jnp.float32).reshape(rows, mixing_values_divided, CHANNELS_ONE_HEAD)
    value_heads = value_rows.astype(jnp.float32).reshape(rows, mixing_values_divided, CHANNELS_ONE_HEAD)
    tail_keys = key_heads.transpose(1, 0, 2) * jnp.exp(suffix_excl) * in_tail[None, :, None]
    end_state = jnp.einsum("hsc,shv->hcv", tail_keys, value_heads, precision=highest)
    decay_total = jnp.all(jnp.logical_not(is_start)).astype(jnp.float32) * jnp.exp(decay_sum)
    _, (outs, from_start) = lax.scan(block_step, init, inputs)

    packed = jnp.concatenate([end_state, decay_total[:, None, :]], axis=1)

    def fold(pieces):
        state, decay = pieces[0][:, :CHANNELS_ONE_HEAD], pieces[0][:, CHANNELS_ONE_HEAD:]
        for piece in pieces[1:]:
            piece_decay = piece[:, CHANNELS_ONE_HEAD:]
            state = jnp.transpose(piece_decay, (0, 2, 1)) * state + piece[:, :CHANNELS_ONE_HEAD]
            decay = piece_decay * decay
        return jnp.concatenate([state, decay], axis=1)

    devices = size_of(SEQ)
    radix = 4
    prefix = fold([from_behind(packed, SEQ, distance) for distance in range(radix, 0, -1)])
    window = radix
    while window < devices:
        behind = [from_behind(prefix, SEQ, window * step) for step in range(radix - 1, 0, -1)]
        prefix = fold(behind + [prefix])
        window *= radix
    incoming = prefix[:, :CHANNELS_ONE_HEAD]
    outs = outs + jnp.einsum("bhtc,hcv->bhtv", from_start, incoming, precision=highest)
    wkv = outs.transpose(0, 2, 1, 3).reshape(rows, mixing_values_divided, CHANNELS_ONE_HEAD)
    mean = jnp.mean(wkv, axis=-1, keepdims=True)
    centred = wkv - mean
    spread = jnp.mean(centred * centred, axis=-1, keepdims=True)
    grouped = (centred * lax.rsqrt(spread + 0.00064)).reshape(
        rows, local_width
    ) * cluster_standardize_scale + cluster_standardize_offset
    gated = (grouped * gate.astype(jnp.float32)).astype(jnp.bfloat16)
    partial_sum = jnp.dot(gated, emitted_mapping_matrix, preferred_element_type=jnp.float32)
    parts = lax.axis_size("tp")
    pieces = partial_sum.astype(jnp.bfloat16).reshape(rows, parts, local_width).transpose(1, 0, 2)
    pieces = lax.all_to_all(pieces, "tp", 0, 0, tiled=True)
    mine = jnp.sum(pieces.astype(jnp.float32), axis=0)
    return (tier_source_concatenated.astype(jnp.float32) + mine).astype(jnp.bfloat16)


def solution(mesh):
    groups = 8 if mesh.shape["seq"] % 8 == 0 else 1
    devices = mesh.devices.reshape(mesh.shape["seq"] // groups, groups, mesh.shape["tp"])
    mesh = jax.sharding.Mesh(devices, ("seq_hi", "seq_lo", "tp"))
    in_specs = (
        P(SEQ, "tp"),
        P(),
        P(),
        P(),
        P(),
        P(None, None, "tp"),
        P(),
        P(None, "tp"),
        P("tp"),
        P("tp"),
        P("tp"),
        P("tp"),
        P("tp", None),
    )
    out_specs = P(SEQ, "tp")
    return jax.shard_map(body, mesh=mesh, in_specs=in_specs, out_specs=out_specs, check_vma=False)
```

```python
import math

import jax
import jax.numpy as jnp
from jax import lax
from jax.sharding import PartitionSpec as P

CHANNELS_ONE_HEAD = 64


highest = lax.Precision.HIGHEST


SEQ = ("seq_hi", "seq_lo")


def size_of(axes):
    return math.prod(lax.axis_size(axis) for axis in axes)


def from_behind(block, axis, distance):
    devices = range(size_of(axis))
    route = [(i - distance, i) for i in devices if i - distance in devices]
    return lax.ppermute(block, axis, route)


def layer_norm(rows, gain, bias, eps):
    mean = jnp.mean(rows, axis=-1, keepdims=True)
    centred = rows - mean
    spread = jnp.mean(centred * centred, axis=-1, keepdims=True)
    return centred * lax.rsqrt(spread + eps) * gain + bias


def body(
    tier_source_concatenated,
    prompt_sizes_ordered,
    tier_standardize_scale,
    tier_standardize_offset,
    previous_item_mixers,
    mapping_matrices_pile,
    fading_narrow_left,
    fading_narrow_right,
    feature_fading_baseline,
    diagonal_boost_coefficient,
    cluster_standardize_scale,
    cluster_standardize_offset,
    emitted_mapping_matrix,
):
    rows = tier_source_concatenated.shape[0]
    local_width = mapping_matrices_pile.shape[2]
    mixing_values_divided = local_width // CHANNELS_ONE_HEAD
    block = min(32, rows)
    blocks = rows // block
    full = lax.all_gather(tier_source_concatenated, "tp", axis=1, tiled=True)
    normed = layer_norm(
        full.astype(jnp.float32), tier_standardize_scale, tier_standardize_offset, 1e-05
    ).astype(jnp.bfloat16)
    first = jnp.cumsum(prompt_sizes_ordered) - prompt_sizes_ordered
    position = lax.axis_index(SEQ) * rows + jnp.arange(rows, dtype=jnp.int32)
    is_start = jnp.any(position[:, None] == first[None, :], axis=1)
    segment = jnp.sum((first[None, :] <= position[:, None]).astype(jnp.int32), axis=1)
    edge = from_behind(normed[rows - 1 :], SEQ, 1)
    previous = jnp.concatenate([edge, normed[: rows - 1]], axis=0)
    previous = jnp.where(is_start[:, None], jnp.zeros_like(previous), previous)
    base = normed.astype(jnp.float32)
    delta = previous.astype(jnp.float32) - base
    shifted_blend = (base[None] + delta[None] * previous_item_mixers[:, None, :]).astype(
        jnp.bfloat16
    )
    projected = jnp.einsum(
        "itd,ide->ite", shifted_blend[:4], mapping_matrices_pile, preferred_element_type=jnp.float32
    )
    recept = projected[0].astype(jnp.bfloat16)
    key_rows = projected[1].astype(jnp.bfloat16)
    value_rows = projected[2].astype(jnp.bfloat16)
    gate = jax.nn.silu(projected[3]).astype(jnp.bfloat16)
    lowrank_decay_delta = jnp.tanh(
        jnp.dot(shifted_blend[4], fading_narrow_left, preferred_element_type=jnp.float32)
    ).astype(jnp.bfloat16)
    decay_logarithm = -feature_fading_baseline[None, :] * jnp.exp(
        jnp.dot(lowrank_decay_delta, fading_narrow_right, preferred_element_type=jnp.float32)
    )

    def split_heads(values):
        return (
            values.astype(jnp.float32)
            .reshape(blocks, block, mixing_values_divided, CHANNELS_ONE_HEAD)
            .transpose(0, 2, 1, 3)
        )

    inputs = (
        split_heads(recept),
        split_heads(key_rows),
        split_heads(value_rows),
        split_heads(decay_logarithm),
        segment.reshape(blocks, block),
        is_start.astype(jnp.float32).reshape(blocks, block),
    )
    order = jnp.arange(block)
    lower_incl = (order[None, :] <= order[:, None]).astype(jnp.float32)
    strictly = order[None, :] < order[:, None]
    diagonal_extra_contribution = diagonal_boost_coefficient.reshape(
        mixing_values_divided, CHANNELS_ONE_HEAD
    )

    gating_rows_tile, query_array_tile, content_slab, lw_b, seg_b, start_b = inputs
    incl = jnp.einsum("ts,bhsc->bhtc", lower_incl, lw_b, precision=highest)
    excl = incl - lw_b
    pair_ok = strictly[None] & (seg_b[:, None, :] == seg_b[:, :, None])
    gap = jnp.minimum(excl[:, :, :, None, :] - incl[:, :, None, :, :], 0.0)
    weight = jnp.where(pair_ok[:, None, :, :, None], jnp.exp(gap), 0.0)
    scores = jnp.einsum(
        "bhtc,bhsc,bhtsc->bhts", gating_rows_tile, query_array_tile, weight, precision=highest
    )
    present_item_reward = jnp.sum(
        gating_rows_tile * diagonal_extra_contribution[None, :, None, :] * query_array_tile, axis=-1
    )
    seen = jnp.einsum("ts,bs->bt", lower_incl, start_b, precision=highest)
    valid = (seen == 0.0).astype(jnp.float32)
    carried = gating_rows_tile * jnp.exp(excl) * valid[:, None, :, None]
    intra = (
        jnp.einsum("bhts,bhsv->bhtv", scores, content_slab, precision=highest)
        + present_item_reward[..., None] * content_slab
    )
    total = incl[:, :, block - 1, :]
    keep = (seen[:, block - 1] == 0.0).astype(jnp.float32)
    tail_ok = (seg_b == seg_b[:, block - 1 :]).astype(jnp.float32)
    tail = query_array_tile * jnp.exp(total[:, :, None, :] - incl) * tail_ok[:, None, :, None]
    block_state = jnp.einsum("bhsc,bhsv->bhcv", tail, content_slab, precision=highest)
    block_decay = keep[:, None, None] * jnp.exp(total)

    state = jnp.zeros_like(block_state[0])
    offset = jnp.zeros_like(total[0])
    alive = jnp.float32(1.0)
    entering, reach = [], []
    for index in range(blocks):
        entering.append(state)
        reach.append(alive * jnp.exp(offset))
        state = block_decay[index][:, :, None] * state + block_state[index]
        offset = offset + total[index]
        alive = alive * keep[index]
    entering = jnp.stack(entering)
    from_start = carried * jnp.stack(reach)[:, :, None, :]
    outs = intra + jnp.einsum("bhtc,bhcv->bhtv", carried, entering, precision=highest)
    end_state = state
    decay_total = alive * jnp.exp(offset)

    packed = jnp.concatenate([end_state, decay_total[:, None, :]], axis=1)

    def combine(received, own):
        own_state, own_decay = own[:, :CHANNELS_ONE_HEAD], own[:, CHANNELS_ONE_HEAD:]
        got_state, got_decay = received[:, :CHANNELS_ONE_HEAD], received[:, CHANNELS_ONE_HEAD:]
        state = jnp.transpose(own_decay, (0, 2, 1)) * got_state + own_state
        return jnp.concatenate([state, own_decay * got_decay], axis=1)

    devices = size_of(SEQ)
    prefix = from_behind(packed, SEQ, 1)
    distance = 1
    while distance < devices:
        prefix = combine(from_behind(prefix, SEQ, distance), prefix)
        distance *= 2
    incoming = prefix[:, :CHANNELS_ONE_HEAD]
    outs = outs + jnp.einsum("bhtc,hcv->bhtv", from_start, incoming, precision=highest)
    wkv = outs.transpose(0, 2, 1, 3).reshape(rows, mixing_values_divided, CHANNELS_ONE_HEAD)
    mean = jnp.mean(wkv, axis=-1, keepdims=True)
    centred = wkv - mean
    spread = jnp.mean(centred * centred, axis=-1, keepdims=True)
    grouped = (centred * lax.rsqrt(spread + 0.00064)).reshape(
        rows, local_width
    ) * cluster_standardize_scale + cluster_standardize_offset
    gated = (grouped * gate.astype(jnp.float32)).astype(jnp.bfloat16)
    partial_sum = jnp.dot(gated, emitted_mapping_matrix, preferred_element_type=jnp.float32)
    parts = lax.axis_size("tp")
    pieces = partial_sum.astype(jnp.bfloat16).reshape(rows, parts, local_width).transpose(1, 0, 2)
    pieces = lax.all_to_all(pieces, "tp", 0, 0, tiled=True)
    mine = jnp.sum(pieces.astype(jnp.float32), axis=0)
    return (tier_source_concatenated.astype(jnp.float32) + mine).astype(jnp.bfloat16)


def solution(mesh):
    groups = 8 if mesh.shape["seq"] % 8 == 0 else 1
    devices = mesh.devices.reshape(mesh.shape["seq"] // groups, groups, mesh.shape["tp"])
    mesh = jax.sharding.Mesh(devices, ("seq_hi", "seq_lo", "tp"))
    in_specs = (
        P(SEQ, "tp"),
        P(),
        P(),
        P(),
        P(),
        P(None, None, "tp"),
        P(),
        P(None, "tp"),
        P("tp"),
        P("tp"),
        P("tp"),
        P("tp"),
        P("tp", None),
    )
    out_specs = P(SEQ, "tp")
    return jax.shard_map(body, mesh=mesh, in_specs=in_specs, out_specs=out_specs, check_vma=False)
```

```python
import math

import jax
import jax.numpy as jnp
from jax import lax
from jax.sharding import PartitionSpec as P

CHANNELS_ONE_HEAD = 64


highest = lax.Precision.HIGHEST


SEQ = ("seq_hi", "seq_lo")


def size_of(axes):
    return math.prod(lax.axis_size(axis) for axis in axes)


def from_behind(block, axis, distance):
    devices = range(size_of(axis))
    route = [(i - distance, i) for i in devices if i - distance in devices]
    return lax.ppermute(block, axis, route)


def layer_norm(rows, gain, bias, eps):
    mean = jnp.mean(rows, axis=-1, keepdims=True)
    centred = rows - mean
    spread = jnp.mean(centred * centred, axis=-1, keepdims=True)
    return centred * lax.rsqrt(spread + eps) * gain + bias


def body(
    tier_source_concatenated,
    prompt_sizes_ordered,
    tier_standardize_scale,
    tier_standardize_offset,
    previous_item_mixers,
    mapping_matrices_pile,
    fading_narrow_left,
    fading_narrow_right,
    feature_fading_baseline,
    diagonal_boost_coefficient,
    cluster_standardize_scale,
    cluster_standardize_offset,
    emitted_mapping_matrix,
):
    rows = tier_source_concatenated.shape[0]
    local_width = mapping_matrices_pile.shape[2]
    mixing_values_divided = local_width // CHANNELS_ONE_HEAD
    block = min(32, rows)
    blocks = rows // block
    full = lax.all_gather(tier_source_concatenated, "tp", axis=1, tiled=True)
    normed = layer_norm(
        full.astype(jnp.float32), tier_standardize_scale, tier_standardize_offset, 1e-05
    ).astype(jnp.bfloat16)
    first = jnp.cumsum(prompt_sizes_ordered) - prompt_sizes_ordered
    position = lax.axis_index(SEQ) * rows + jnp.arange(rows, dtype=jnp.int32)
    is_start = jnp.any(position[:, None] == first[None, :], axis=1)
    segment = jnp.sum((first[None, :] <= position[:, None]).astype(jnp.int32), axis=1)
    edge = from_behind(normed[rows - 1 :], SEQ, 1)
    previous = jnp.concatenate([edge, normed[: rows - 1]], axis=0)
    previous = jnp.where(is_start[:, None], jnp.zeros_like(previous), previous)
    base = normed.astype(jnp.float32)
    delta = previous.astype(jnp.float32) - base
    shifted_blend = (base[None] + delta[None] * previous_item_mixers[:, None, :]).astype(
        jnp.bfloat16
    )
    projected = jnp.einsum(
        "itd,ide->ite", shifted_blend[:4], mapping_matrices_pile, preferred_element_type=jnp.float32
    )
    recept = projected[0].astype(jnp.bfloat16)
    key_rows = projected[1].astype(jnp.bfloat16)
    value_rows = projected[2].astype(jnp.bfloat16)
    gate = jax.nn.silu(projected[3]).astype(jnp.bfloat16)
    lowrank_decay_delta = jnp.tanh(
        jnp.dot(shifted_blend[4], fading_narrow_left, preferred_element_type=jnp.float32)
    ).astype(jnp.bfloat16)
    decay_logarithm = -feature_fading_baseline[None, :] * jnp.exp(
        jnp.dot(lowrank_decay_delta, fading_narrow_right, preferred_element_type=jnp.float32)
    )

    def split_heads(values):
        return (
            values.astype(jnp.float32)
            .reshape(blocks, block, mixing_values_divided, CHANNELS_ONE_HEAD)
            .transpose(0, 2, 1, 3)
        )

    inputs = (
        split_heads(recept),
        split_heads(key_rows),
        split_heads(value_rows),
        split_heads(decay_logarithm),
        segment.reshape(blocks, block),
        is_start.astype(jnp.float32).reshape(blocks, block),
    )
    order = jnp.arange(block)
    lower_incl = (order[None, :] <= order[:, None]).astype(jnp.float32)
    strictly = order[None, :] < order[:, None]
    diagonal_extra_contribution = diagonal_boost_coefficient.reshape(
        mixing_values_divided, CHANNELS_ONE_HEAD
    )

    gating_rows_tile, query_array_tile, content_slab, lw_b, seg_b, start_b = inputs
    incl = jnp.einsum("ts,bhsc->bhtc", lower_incl, lw_b, precision=highest)
    excl = incl - lw_b
    pair_ok = strictly[None] & (seg_b[:, None, :] == seg_b[:, :, None])
    gap = jnp.minimum(excl[:, :, :, None, :] - incl[:, :, None, :, :], 0.0)
    weight = jnp.where(pair_ok[:, None, :, :, None], jnp.exp(gap), 0.0)
    scores = jnp.einsum(
        "bhtc,bhsc,bhtsc->bhts", gating_rows_tile, query_array_tile, weight, precision=highest
    )
    present_item_reward = jnp.sum(
        gating_rows_tile * diagonal_extra_contribution[None, :, None, :] * query_array_tile, axis=-1
    )
    seen = jnp.einsum("ts,bs->bt", lower_incl, start_b, precision=highest)
    valid = (seen == 0.0).astype(jnp.float32)
    carried = gating_rows_tile * jnp.exp(excl) * valid[:, None, :, None]
    intra = (
        jnp.einsum("bhts,bhsv->bhtv", scores, content_slab, precision=highest)
        + present_item_reward[..., None] * content_slab
    )
    total = incl[:, :, block - 1, :]
    keep = (seen[:, block - 1] == 0.0).astype(jnp.float32)
    tail_ok = (seg_b == seg_b[:, block - 1 :]).astype(jnp.float32)
    tail = query_array_tile * jnp.exp(total[:, :, None, :] - incl) * tail_ok[:, None, :, None]
    block_state = jnp.einsum("bhsc,bhsv->bhcv", tail, content_slab, precision=highest)
    block_decay = keep[:, None, None] * jnp.exp(total)

    state = jnp.zeros_like(block_state[0])
    offset = jnp.zeros_like(total[0])
    alive = jnp.float32(1.0)
    entering, reach = [], []
    for index in range(blocks):
        entering.append(state)
        reach.append(alive * jnp.exp(offset))
        state = block_decay[index][:, :, None] * state + block_state[index]
        offset = offset + total[index]
        alive = alive * keep[index]
    entering = jnp.stack(entering)
    from_start = carried * jnp.stack(reach)[:, :, None, :]
    outs = intra + jnp.einsum("bhtc,bhcv->bhtv", carried, entering, precision=highest)
    end_state = state
    decay_total = alive * jnp.exp(offset)

    lanes = 128 if (mixing_values_divided * CHANNELS_ONE_HEAD) % 128 == 0 else CHANNELS_ONE_HEAD
    state_rows = end_state.size // lanes

    def pack(state, decay):
        return jnp.concatenate([state.reshape(-1, lanes), decay.reshape(-1, lanes)], axis=0)

    def combine(received, own):
        own_state = own[:state_rows].reshape(end_state.shape)
        own_decay = own[state_rows:].reshape(decay_total.shape)
        got_state = received[:state_rows].reshape(end_state.shape)
        got_decay = received[state_rows:].reshape(decay_total.shape)
        return pack(own_decay[:, :, None] * got_state + own_state, own_decay * got_decay)

    devices = size_of(SEQ)
    prefix = pack(end_state, decay_total)
    distance = 1
    while 2 * distance < devices:
        prefix = combine(from_behind(prefix, SEQ, distance), prefix)
        distance *= 2
    prefix = combine(from_behind(prefix, SEQ, distance + 1), from_behind(prefix, SEQ, 1))
    incoming = prefix[:state_rows].reshape(end_state.shape)
    outs = outs + jnp.einsum("bhtc,hcv->bhtv", from_start, incoming, precision=highest)
    wkv = outs.transpose(0, 2, 1, 3).reshape(rows, mixing_values_divided, CHANNELS_ONE_HEAD)
    mean = jnp.mean(wkv, axis=-1, keepdims=True)
    centred = wkv - mean
    spread = jnp.mean(centred * centred, axis=-1, keepdims=True)
    grouped = (centred * lax.rsqrt(spread + 0.00064)).reshape(
        rows, local_width
    ) * cluster_standardize_scale + cluster_standardize_offset
    gated = (grouped * gate.astype(jnp.float32)).astype(jnp.bfloat16)
    partial_sum = jnp.dot(gated, emitted_mapping_matrix, preferred_element_type=jnp.float32)
    parts = lax.axis_size("tp")
    pieces = partial_sum.astype(jnp.bfloat16).reshape(rows, parts, local_width).transpose(1, 0, 2)
    pieces = lax.all_to_all(pieces, "tp", 0, 0, tiled=True)
    mine = jnp.sum(pieces.astype(jnp.float32), axis=0)
    return (tier_source_concatenated.astype(jnp.float32) + mine).astype(jnp.bfloat16)


def solution(mesh):
    groups = 8 if mesh.shape["seq"] % 8 == 0 else 1
    devices = mesh.devices.reshape(mesh.shape["seq"] // groups, groups, mesh.shape["tp"])
    mesh = jax.sharding.Mesh(devices, ("seq_hi", "seq_lo", "tp"))
    in_specs = (
        P(SEQ, "tp"),
        P(),
        P(),
        P(),
        P(),
        P(None, None, "tp"),
        P(),
        P(None, "tp"),
        P("tp"),
        P("tp"),
        P("tp"),
        P("tp"),
        P("tp", None),
    )
    out_specs = P(SEQ, "tp")
    return jax.shard_map(body, mesh=mesh, in_specs=in_specs, out_specs=out_specs, check_vma=False)
```

```python
import math

import jax
import jax.numpy as jnp
from jax import lax
from jax.sharding import PartitionSpec as P

CHANNELS_ONE_HEAD = 64


highest = lax.Precision.HIGHEST


SEQ = ("seq_hi", "seq_lo")


def size_of(axes):
    return math.prod(lax.axis_size(axis) for axis in axes)


def from_behind(block, axis, distance):
    devices = range(size_of(axis))
    route = [(i - distance, i) for i in devices if i - distance in devices]
    return lax.ppermute(block, axis, route)


def layer_norm(rows, gain, bias, eps):
    mean = jnp.mean(rows, axis=-1, keepdims=True)
    centred = rows - mean
    spread = jnp.mean(centred * centred, axis=-1, keepdims=True)
    return centred * lax.rsqrt(spread + eps) * gain + bias


def body(
    tier_source_concatenated,
    prompt_sizes_ordered,
    tier_standardize_scale,
    tier_standardize_offset,
    previous_item_mixers,
    mapping_matrices_pile,
    fading_narrow_left,
    fading_narrow_right,
    feature_fading_baseline,
    diagonal_boost_coefficient,
    cluster_standardize_scale,
    cluster_standardize_offset,
    emitted_mapping_matrix,
):
    rows = tier_source_concatenated.shape[0]
    local_width = mapping_matrices_pile.shape[2]
    mixing_values_divided = local_width // CHANNELS_ONE_HEAD
    block = min(32, rows)
    blocks = rows // block
    full = lax.all_gather(tier_source_concatenated, "tp", axis=1, tiled=True)
    normed = layer_norm(
        full.astype(jnp.float32), tier_standardize_scale, tier_standardize_offset, 1e-05
    ).astype(jnp.bfloat16)
    first = jnp.cumsum(prompt_sizes_ordered) - prompt_sizes_ordered
    position = lax.axis_index(SEQ) * rows + jnp.arange(rows, dtype=jnp.int32)
    is_start = jnp.any(position[:, None] == first[None, :], axis=1)
    segment = jnp.sum((first[None, :] <= position[:, None]).astype(jnp.int32), axis=1)
    def blend(previous, rows_normed):
        base = rows_normed.astype(jnp.float32)
        delta = previous.astype(jnp.float32) - base
        return (base[None] + delta[None] * previous_item_mixers[:, None, :]).astype(jnp.bfloat16)

    def project(mixed):
        return (
            jnp.einsum(
                "itd,ide->ite", mixed[:4], mapping_matrices_pile, preferred_element_type=jnp.float32
            ),
            jnp.dot(mixed[4], fading_narrow_left, preferred_element_type=jnp.float32),
        )

    previous = jnp.concatenate([jnp.zeros_like(normed[:1]), normed[: rows - 1]], axis=0)
    previous = jnp.where(is_start[:, None], jnp.zeros_like(previous), previous)
    projected, lowrank = project(blend(previous, normed))
    edge = from_behind(normed[rows - 1 :], SEQ, 1)
    edge = jnp.where(is_start[0], jnp.zeros_like(edge), edge)
    edge_projected, edge_lowrank = project(blend(edge, normed[:1]))
    projected = lax.dynamic_update_slice(projected, edge_projected, (0, 0, 0))
    lowrank = lax.dynamic_update_slice(lowrank, edge_lowrank, (0, 0))
    recept = projected[0].astype(jnp.bfloat16)
    key_rows = projected[1].astype(jnp.bfloat16)
    value_rows = projected[2].astype(jnp.bfloat16)
    gate = jax.nn.silu(projected[3]).astype(jnp.bfloat16)
    lowrank_decay_delta = jnp.tanh(lowrank).astype(jnp.bfloat16)
    decay_logarithm = -feature_fading_baseline[None, :] * jnp.exp(
        jnp.dot(lowrank_decay_delta, fading_narrow_right, preferred_element_type=jnp.float32)
    )

    def split_heads(values):
        return (
            values.astype(jnp.float32)
            .reshape(blocks, block, mixing_values_divided, CHANNELS_ONE_HEAD)
            .transpose(0, 2, 1, 3)
        )

    inputs = (
        split_heads(recept),
        split_heads(key_rows),
        split_heads(value_rows),
        split_heads(decay_logarithm),
        segment.reshape(blocks, block),
        is_start.astype(jnp.float32).reshape(blocks, block),
    )
    order = jnp.arange(block)
    lower_incl = (order[None, :] <= order[:, None]).astype(jnp.float32)
    strictly = order[None, :] < order[:, None]
    diagonal_extra_contribution = diagonal_boost_coefficient.reshape(
        mixing_values_divided, CHANNELS_ONE_HEAD
    )

    gating_rows_tile, query_array_tile, content_slab, lw_b, seg_b, start_b = inputs
    incl = jnp.einsum("ts,bhsc->bhtc", lower_incl, lw_b, precision=highest)
    excl = incl - lw_b
    present_item_reward = jnp.sum(
        gating_rows_tile * diagonal_extra_contribution[None, :, None, :] * query_array_tile, axis=-1
    )
    seen = jnp.einsum("ts,bs->bt", lower_incl, start_b, precision=highest)
    valid = (seen == 0.0).astype(jnp.float32)
    carried = gating_rows_tile * jnp.exp(excl) * valid[:, None, :, None]
    total = incl[:, :, block - 1, :]
    keep = (seen[:, block - 1] == 0.0).astype(jnp.float32)
    tail_ok = (seg_b == seg_b[:, block - 1 :]).astype(jnp.float32)
    tail = query_array_tile * jnp.exp(total[:, :, None, :] - incl) * tail_ok[:, None, :, None]
    block_state = jnp.einsum("bhsc,bhsv->bhcv", tail, content_slab, precision=highest)
    block_decay = keep[:, None, None] * jnp.exp(total)

    state = jnp.zeros_like(block_state[0])
    offset = jnp.zeros_like(total[0])
    alive = jnp.float32(1.0)
    entering, reach = [], []
    for index in range(blocks):
        entering.append(state)
        reach.append(alive * jnp.exp(offset))
        state = block_decay[index][:, :, None] * state + block_state[index]
        offset = offset + total[index]
        alive = alive * keep[index]
    entering = jnp.stack(entering)
    from_start = carried * jnp.stack(reach)[:, :, None, :]
    end_state = state
    decay_total = alive * jnp.exp(offset)

    packed = jnp.concatenate([end_state, decay_total[:, None, :]], axis=1)

    def combine(received, own):
        own_state, own_decay = own[:, :CHANNELS_ONE_HEAD], own[:, CHANNELS_ONE_HEAD:]
        got_state, got_decay = received[:, :CHANNELS_ONE_HEAD], received[:, CHANNELS_ONE_HEAD:]
        state = jnp.transpose(own_decay, (0, 2, 1)) * got_state + own_state
        return jnp.concatenate([state, own_decay * got_decay], axis=1)

    devices = size_of(SEQ)
    def block_scores(index, incl_b, excl_b, recept_b, key_b):
        pair_ok = strictly & (seg_b[index][None, :] == seg_b[index][:, None])
        gap = jnp.minimum(excl_b[:, :, None, :] - incl_b[:, None, :, :], 0.0)
        weight = jnp.where(pair_ok[None, :, :, None], jnp.exp(gap), 0.0)
        return jnp.einsum("htc,hsc,htsc->hts", recept_b, key_b, weight, precision=highest)

    scores = []
    prefix = from_behind(packed, SEQ, 1)
    distance = 1
    while distance < devices:
        prefix = combine(from_behind(prefix, SEQ, distance), prefix)
        distance *= 2
        index = len(scores)
        if index < blocks:
            operands = (incl[index], excl[index], gating_rows_tile[index], query_array_tile[index])
            prefix, operands = lax.optimization_barrier((prefix, operands))
            scores.append(block_scores(index, *operands))
    for index in range(len(scores), blocks):
        scores.append(
            block_scores(index, incl[index], excl[index], gating_rows_tile[index], query_array_tile[index])
        )
    scores = jnp.stack(scores)
    outs = (
        jnp.einsum("bhts,bhsv->bhtv", scores, content_slab, precision=highest)
        + present_item_reward[..., None] * content_slab
        + jnp.einsum("bhtc,bhcv->bhtv", carried, entering, precision=highest)
    )
    incoming = prefix[:, :CHANNELS_ONE_HEAD]
    outs = outs + jnp.einsum("bhtc,hcv->bhtv", from_start, incoming, precision=highest)
    wkv = outs.transpose(0, 2, 1, 3).reshape(rows, mixing_values_divided, CHANNELS_ONE_HEAD)
    mean = jnp.mean(wkv, axis=-1, keepdims=True)
    centred = wkv - mean
    spread = jnp.mean(centred * centred, axis=-1, keepdims=True)
    grouped = (centred * lax.rsqrt(spread + 0.00064)).reshape(
        rows, local_width
    ) * cluster_standardize_scale + cluster_standardize_offset
    gated = (grouped * gate.astype(jnp.float32)).astype(jnp.bfloat16)
    partial_sum = jnp.dot(gated, emitted_mapping_matrix, preferred_element_type=jnp.float32)
    parts = lax.axis_size("tp")
    pieces = partial_sum.astype(jnp.bfloat16).reshape(rows, parts, local_width).transpose(1, 0, 2)
    pieces = lax.all_to_all(pieces, "tp", 0, 0, tiled=True)
    mine = jnp.sum(pieces.astype(jnp.float32), axis=0)
    return (tier_source_concatenated.astype(jnp.float32) + mine).astype(jnp.bfloat16)


def solution(mesh):
    groups = 8 if mesh.shape["seq"] % 8 == 0 else 1
    devices = mesh.devices.reshape(mesh.shape["seq"] // groups, groups, mesh.shape["tp"])
    mesh = jax.sharding.Mesh(devices, ("seq_hi", "seq_lo", "tp"))
    in_specs = (
        P(SEQ, "tp"),
        P(),
        P(),
        P(),
        P(),
        P(None, None, "tp"),
        P(),
        P(None, "tp"),
        P("tp"),
        P("tp"),
        P("tp"),
        P("tp"),
        P("tp", None),
    )
    out_specs = P(SEQ, "tp")
    return jax.shard_map(body, mesh=mesh, in_specs=in_specs, out_specs=out_specs, check_vma=False)
```

```python
import math

import jax
import jax.numpy as jnp
from jax import lax
from jax.sharding import PartitionSpec as P

CHANNELS_ONE_HEAD = 64


highest = lax.Precision.HIGHEST


SEQ = ("seq_hi", "seq_lo")


def size_of(axes):
    return math.prod(lax.axis_size(axis) for axis in axes)


def from_behind(block, axis, distance):
    devices = range(size_of(axis))
    route = [(i - distance, i) for i in devices if i - distance in devices]
    return lax.ppermute(block, axis, route)


def layer_norm(rows, gain, bias, eps):
    mean = jnp.mean(rows, axis=-1, keepdims=True)
    centred = rows - mean
    spread = jnp.mean(centred * centred, axis=-1, keepdims=True)
    return centred * lax.rsqrt(spread + eps) * gain + bias


def body(
    tier_source_concatenated,
    prompt_sizes_ordered,
    tier_standardize_scale,
    tier_standardize_offset,
    previous_item_mixers,
    mapping_matrices_pile,
    fading_narrow_left,
    fading_narrow_right,
    feature_fading_baseline,
    diagonal_boost_coefficient,
    cluster_standardize_scale,
    cluster_standardize_offset,
    emitted_mapping_matrix,
):
    rows = tier_source_concatenated.shape[0]
    local_width = mapping_matrices_pile.shape[2]
    mixing_values_divided = local_width // CHANNELS_ONE_HEAD
    block = min(32, rows)
    blocks = rows // block
    full = lax.all_gather(tier_source_concatenated, "tp", axis=1, tiled=True)
    normed = layer_norm(
        full.astype(jnp.float32), tier_standardize_scale, tier_standardize_offset, 1e-05
    ).astype(jnp.bfloat16)
    first = jnp.cumsum(prompt_sizes_ordered) - prompt_sizes_ordered
    position = lax.axis_index(SEQ) * rows + jnp.arange(rows, dtype=jnp.int32)
    is_start = jnp.any(position[:, None] == first[None, :], axis=1)
    segment = jnp.sum((first[None, :] <= position[:, None]).astype(jnp.int32), axis=1)
    def blend(previous, rows_normed):
        base = rows_normed.astype(jnp.float32)
        delta = previous.astype(jnp.float32) - base
        return (base[None] + delta[None] * previous_item_mixers[:, None, :]).astype(jnp.bfloat16)

    def project(mixed, index):
        return jnp.dot(mixed[index], mapping_matrices_pile[index], preferred_element_type=jnp.float32)

    def fixed(index, mixed, edge_mixed):
        return lax.dynamic_update_slice(project(mixed, index), project(edge_mixed, index), (0, 0))

    previous = jnp.concatenate([jnp.zeros_like(normed[:1]), normed[: rows - 1]], axis=0)
    previous = jnp.where(is_start[:, None], jnp.zeros_like(previous), previous)
    mixed = blend(previous, normed)
    edge = from_behind(normed[rows - 1 :], SEQ, 1)
    edge = jnp.where(is_start[0], jnp.zeros_like(edge), edge)
    edge_mixed = blend(edge, normed[:1])
    key_rows = fixed(1, mixed, edge_mixed).astype(jnp.bfloat16)
    value_rows = fixed(2, mixed, edge_mixed).astype(jnp.bfloat16)
    lowrank = lax.dynamic_update_slice(
        jnp.dot(mixed[4], fading_narrow_left, preferred_element_type=jnp.float32),
        jnp.dot(edge_mixed[4], fading_narrow_left, preferred_element_type=jnp.float32),
        (0, 0),
    )
    lowrank_decay_delta = jnp.tanh(lowrank).astype(jnp.bfloat16)
    decay_logarithm = -feature_fading_baseline[None, :] * jnp.exp(
        jnp.dot(lowrank_decay_delta, fading_narrow_right, preferred_element_type=jnp.float32)
    )

    def split_heads(values):
        return (
            values.astype(jnp.float32)
            .reshape(blocks, block, mixing_values_divided, CHANNELS_ONE_HEAD)
            .transpose(0, 2, 1, 3)
        )

    inputs = (
        split_heads(key_rows),
        split_heads(value_rows),
        split_heads(decay_logarithm),
        segment.reshape(blocks, block),
        is_start.astype(jnp.float32).reshape(blocks, block),
    )
    order = jnp.arange(block)
    lower_incl = (order[None, :] <= order[:, None]).astype(jnp.float32)
    strictly = order[None, :] < order[:, None]
    diagonal_extra_contribution = diagonal_boost_coefficient.reshape(
        mixing_values_divided, CHANNELS_ONE_HEAD
    )

    query_array_tile, content_slab, lw_b, seg_b, start_b = inputs
    incl = jnp.einsum("ts,bhsc->bhtc", lower_incl, lw_b, precision=highest)
    excl = incl - lw_b
    seen = jnp.einsum("ts,bs->bt", lower_incl, start_b, precision=highest)
    valid = (seen == 0.0).astype(jnp.float32)
    decay_factor = jnp.exp(excl) * valid[:, None, :, None]
    total = incl[:, :, block - 1, :]
    keep = (seen[:, block - 1] == 0.0).astype(jnp.float32)
    tail_ok = (seg_b == seg_b[:, block - 1 :]).astype(jnp.float32)
    tail = query_array_tile * jnp.exp(total[:, :, None, :] - incl) * tail_ok[:, None, :, None]
    block_state = jnp.einsum("bhsc,bhsv->bhcv", tail, content_slab, precision=highest)
    block_decay = keep[:, None, None] * jnp.exp(total)

    state = jnp.zeros_like(block_state[0])
    offset = jnp.zeros_like(total[0])
    alive = jnp.float32(1.0)
    entering, reach = [], []
    for index in range(blocks):
        entering.append(state)
        reach.append(alive * jnp.exp(offset))
        state = block_decay[index][:, :, None] * state + block_state[index]
        offset = offset + total[index]
        alive = alive * keep[index]
    entering = jnp.stack(entering)
    reach = jnp.stack(reach)[:, :, None, :]
    end_state = state
    decay_total = alive * jnp.exp(offset)

    packed = jnp.concatenate([end_state, decay_total[:, None, :]], axis=1)

    def combine(received, own):
        own_state, own_decay = own[:, :CHANNELS_ONE_HEAD], own[:, CHANNELS_ONE_HEAD:]
        got_state, got_decay = received[:, :CHANNELS_ONE_HEAD], received[:, CHANNELS_ONE_HEAD:]
        state = jnp.transpose(own_decay, (0, 2, 1)) * got_state + own_state
        return jnp.concatenate([state, own_decay * got_decay], axis=1)

    devices = size_of(SEQ)
    def block_scores(index, incl_b, excl_b, recept_b, key_b):
        pair_ok = strictly & (seg_b[index][None, :] == seg_b[index][:, None])
        gap = jnp.minimum(excl_b[:, :, None, :] - incl_b[:, None, :, :], 0.0)
        weight = jnp.where(pair_ok[None, :, :, None], jnp.exp(gap), 0.0)
        return jnp.einsum("htc,hsc,htsc->hts", recept_b, key_b, weight, precision=highest)

    scores = []
    prefix = from_behind(packed, SEQ, 1)
    prefix, late = lax.optimization_barrier((prefix, (mixed, edge_mixed)))
    recept = fixed(0, *late).astype(jnp.bfloat16)
    gate = jax.nn.silu(fixed(3, *late)).astype(jnp.bfloat16)
    gating_rows_tile = split_heads(recept)
    carried = gating_rows_tile * decay_factor
    from_start = carried * reach
    present_item_reward = jnp.sum(
        gating_rows_tile * diagonal_extra_contribution[None, :, None, :] * query_array_tile, axis=-1
    )
    distance = 1
    while distance < devices:
        prefix = combine(from_behind(prefix, SEQ, distance), prefix)
        distance *= 2
        index = len(scores)
        if index < blocks:
            operands = (incl[index], excl[index], gating_rows_tile[index], query_array_tile[index])
            prefix, operands = lax.optimization_barrier((prefix, operands))
            scores.append(block_scores(index, *operands))
    for index in range(len(scores), blocks):
        scores.append(
            block_scores(index, incl[index], excl[index], gating_rows_tile[index], query_array_tile[index])
        )
    scores = jnp.stack(scores)
    outs = (
        jnp.einsum("bhts,bhsv->bhtv", scores, content_slab, precision=highest)
        + present_item_reward[..., None] * content_slab
        + jnp.einsum("bhtc,bhcv->bhtv", carried, entering, precision=highest)
    )
    incoming = prefix[:, :CHANNELS_ONE_HEAD]
    outs = outs + jnp.einsum("bhtc,hcv->bhtv", from_start, incoming, precision=highest)
    wkv = outs.transpose(0, 2, 1, 3).reshape(rows, mixing_values_divided, CHANNELS_ONE_HEAD)
    mean = jnp.mean(wkv, axis=-1, keepdims=True)
    centred = wkv - mean
    spread = jnp.mean(centred * centred, axis=-1, keepdims=True)
    grouped = (centred * lax.rsqrt(spread + 0.00064)).reshape(
        rows, local_width
    ) * cluster_standardize_scale + cluster_standardize_offset
    gated = (grouped * gate.astype(jnp.float32)).astype(jnp.bfloat16)
    partial_sum = jnp.dot(gated, emitted_mapping_matrix, preferred_element_type=jnp.float32)
    parts = lax.axis_size("tp")
    pieces = partial_sum.astype(jnp.bfloat16).reshape(rows, parts, local_width).transpose(1, 0, 2)
    pieces = lax.all_to_all(pieces, "tp", 0, 0, tiled=True)
    mine = jnp.sum(pieces.astype(jnp.float32), axis=0)
    return (tier_source_concatenated.astype(jnp.float32) + mine).astype(jnp.bfloat16)


def solution(mesh):
    groups = 8 if mesh.shape["seq"] % 8 == 0 else 1
    devices = mesh.devices.reshape(mesh.shape["seq"] // groups, groups, mesh.shape["tp"])
    mesh = jax.sharding.Mesh(devices, ("seq_hi", "seq_lo", "tp"))
    in_specs = (
        P(SEQ, "tp"),
        P(),
        P(),
        P(),
        P(),
        P(None, None, "tp"),
        P(),
        P(None, "tp"),
        P("tp"),
        P("tp"),
        P("tp"),
        P("tp"),
        P("tp", None),
    )
    out_specs = P(SEQ, "tp")
    return jax.shard_map(body, mesh=mesh, in_specs=in_specs, out_specs=out_specs, check_vma=False)
```

```python
import math

import jax
import jax.numpy as jnp
from jax import lax
from jax.sharding import PartitionSpec as P

CHANNELS_ONE_HEAD = 64


highest = lax.Precision.HIGHEST


SEQ = ("seq_hi", "seq_lo")


def size_of(axes):
    return math.prod(lax.axis_size(axis) for axis in axes)


def from_behind(block, axis, distance):
    devices = range(size_of(axis))
    route = [(i - distance, i) for i in devices if i - distance in devices]
    return lax.ppermute(block, axis, route)


def layer_norm(rows, gain, bias, eps):
    mean = jnp.mean(rows, axis=-1, keepdims=True)
    centred = rows - mean
    spread = jnp.mean(centred * centred, axis=-1, keepdims=True)
    return centred * lax.rsqrt(spread + eps) * gain + bias


def body(
    tier_source_concatenated,
    prompt_sizes_ordered,
    tier_standardize_scale,
    tier_standardize_offset,
    previous_item_mixers,
    mapping_matrices_pile,
    fading_narrow_left,
    fading_narrow_right,
    feature_fading_baseline,
    diagonal_boost_coefficient,
    cluster_standardize_scale,
    cluster_standardize_offset,
    emitted_mapping_matrix,
):
    rows = tier_source_concatenated.shape[0]
    local_width = mapping_matrices_pile.shape[2]
    mixing_values_divided = local_width // CHANNELS_ONE_HEAD
    block = min(32, rows)
    blocks = rows // block
    full = lax.all_gather(tier_source_concatenated, "tp", axis=1, tiled=True)
    normed = layer_norm(
        full.astype(jnp.float32), tier_standardize_scale, tier_standardize_offset, 1e-05
    ).astype(jnp.bfloat16)
    first = jnp.cumsum(prompt_sizes_ordered) - prompt_sizes_ordered
    position = lax.axis_index(SEQ) * rows + jnp.arange(rows, dtype=jnp.int32)
    is_start = jnp.any(position[:, None] == first[None, :], axis=1)
    segment = jnp.sum((first[None, :] <= position[:, None]).astype(jnp.int32), axis=1)
    def blend(previous, rows_normed):
        base = rows_normed.astype(jnp.float32)
        delta = previous.astype(jnp.float32) - base
        return (base[None] + delta[None] * previous_item_mixers[:, None, :]).astype(jnp.bfloat16)

    def project(mixed):
        return (
            jnp.einsum(
                "itd,ide->ite", mixed[:4], mapping_matrices_pile, preferred_element_type=jnp.float32
            ),
            jnp.dot(mixed[4], fading_narrow_left, preferred_element_type=jnp.float32),
        )

    previous = jnp.concatenate([jnp.zeros_like(normed[:1]), normed[: rows - 1]], axis=0)
    previous = jnp.where(is_start[:, None], jnp.zeros_like(previous), previous)
    projected, lowrank = project(blend(previous, normed))
    edge = from_behind(normed[rows - 1 :], SEQ, 1)
    edge = jnp.where(is_start[0], jnp.zeros_like(edge), edge)
    edge_projected, edge_lowrank = project(blend(edge, normed[:1]))
    projected = lax.dynamic_update_slice(projected, edge_projected, (0, 0, 0))
    lowrank = lax.dynamic_update_slice(lowrank, edge_lowrank, (0, 0))
    recept = projected[0].astype(jnp.bfloat16)
    key_rows = projected[1].astype(jnp.bfloat16)
    value_rows = projected[2].astype(jnp.bfloat16)
    gate = jax.nn.silu(projected[3]).astype(jnp.bfloat16)
    lowrank_decay_delta = jnp.tanh(lowrank).astype(jnp.bfloat16)
    decay_logarithm = -feature_fading_baseline[None, :] * jnp.exp(
        jnp.dot(lowrank_decay_delta, fading_narrow_right, preferred_element_type=jnp.float32)
    )

    def split_heads(values):
        return (
            values.astype(jnp.float32)
            .reshape(blocks, block, mixing_values_divided, CHANNELS_ONE_HEAD)
            .transpose(0, 2, 1, 3)
        )

    inputs = (
        split_heads(recept),
        split_heads(key_rows),
        split_heads(value_rows),
        split_heads(decay_logarithm),
        segment.reshape(blocks, block),
        is_start.astype(jnp.float32).reshape(blocks, block),
    )
    order = jnp.arange(block)
    lower_incl = (order[None, :] <= order[:, None]).astype(jnp.float32)
    strictly = order[None, :] < order[:, None]
    diagonal_extra_contribution = diagonal_boost_coefficient.reshape(
        mixing_values_divided, CHANNELS_ONE_HEAD
    )

    gating_rows_tile, query_array_tile, content_slab, lw_b, seg_b, start_b = inputs
    incl = jnp.einsum("ts,bhsc->bhtc", lower_incl, lw_b, precision=highest)
    excl = incl - lw_b
    present_item_reward = jnp.sum(
        gating_rows_tile * diagonal_extra_contribution[None, :, None, :] * query_array_tile, axis=-1
    )
    seen = jnp.einsum("ts,bs->bt", lower_incl, start_b, precision=highest)
    valid = (seen == 0.0).astype(jnp.float32)
    carried = gating_rows_tile * jnp.exp(excl) * valid[:, None, :, None]
    total = incl[:, :, block - 1, :]
    keep = (seen[:, block - 1] == 0.0).astype(jnp.float32)
    tail_ok = (seg_b == seg_b[:, block - 1 :]).astype(jnp.float32)
    tail = query_array_tile * jnp.exp(total[:, :, None, :] - incl) * tail_ok[:, None, :, None]
    block_state = jnp.einsum("bhsc,bhsv->bhcv", tail, content_slab, precision=highest)
    block_decay = keep[:, None, None] * jnp.exp(total)

    state = jnp.zeros_like(block_state[0])
    offset = jnp.zeros_like(total[0])
    alive = jnp.float32(1.0)
    entering, reach = [], []
    for index in range(blocks):
        entering.append(state)
        reach.append(alive * jnp.exp(offset))
        state = block_decay[index][:, :, None] * state + block_state[index]
        offset = offset + total[index]
        alive = alive * keep[index]
    entering = jnp.stack(entering)
    from_start = carried * jnp.stack(reach)[:, :, None, :]
    end_state = state
    decay_total = alive * jnp.exp(offset)

    packed = jnp.concatenate([end_state, decay_total[:, None, :]], axis=1)

    def combine(received, own):
        own_state, own_decay = own[:, :CHANNELS_ONE_HEAD], own[:, CHANNELS_ONE_HEAD:]
        got_state, got_decay = received[:, :CHANNELS_ONE_HEAD], received[:, CHANNELS_ONE_HEAD:]
        state = jnp.transpose(own_decay, (0, 2, 1)) * got_state + own_state
        return jnp.concatenate([state, own_decay * got_decay], axis=1)

    devices = size_of(SEQ)
    def block_scores(index, incl_b, excl_b, recept_b, key_b):
        pair_ok = strictly & (seg_b[index][None, :] == seg_b[index][:, None])
        gap = jnp.minimum(excl_b[:, :, None, :] - incl_b[:, None, :, :], 0.0)
        weight = jnp.where(pair_ok[None, :, :, None], jnp.exp(gap), 0.0)
        return jnp.einsum("htc,hsc,htsc->hts", recept_b, key_b, weight, precision=highest)

    scores = []
    prefix = packed
    distance = 1
    while 2 * distance < devices:
        prefix = combine(from_behind(prefix, SEQ, distance), prefix)
        distance *= 2
        index = len(scores)
        if index < blocks:
            operands = (incl[index], excl[index], gating_rows_tile[index], query_array_tile[index])
            prefix, operands = lax.optimization_barrier((prefix, operands))
            scores.append(block_scores(index, *operands))
    prefix = combine(from_behind(prefix, SEQ, distance + 1), from_behind(prefix, SEQ, 1))
    for index in range(len(scores), blocks):
        scores.append(
            block_scores(index, incl[index], excl[index], gating_rows_tile[index], query_array_tile[index])
        )
    scores = jnp.stack(scores)
    outs = (
        jnp.einsum("bhts,bhsv->bhtv", scores, content_slab, precision=highest)
        + present_item_reward[..., None] * content_slab
        + jnp.einsum("bhtc,bhcv->bhtv", carried, entering, precision=highest)
    )
    incoming = prefix[:, :CHANNELS_ONE_HEAD]
    outs = outs + jnp.einsum("bhtc,hcv->bhtv", from_start, incoming, precision=highest)
    wkv = outs.transpose(0, 2, 1, 3).reshape(rows, mixing_values_divided, CHANNELS_ONE_HEAD)
    mean = jnp.mean(wkv, axis=-1, keepdims=True)
    centred = wkv - mean
    spread = jnp.mean(centred * centred, axis=-1, keepdims=True)
    grouped = (centred * lax.rsqrt(spread + 0.00064)).reshape(
        rows, local_width
    ) * cluster_standardize_scale + cluster_standardize_offset
    gated = (grouped * gate.astype(jnp.float32)).astype(jnp.bfloat16)
    partial_sum = jnp.dot(gated, emitted_mapping_matrix, preferred_element_type=jnp.float32)
    parts = lax.axis_size("tp")
    pieces = partial_sum.astype(jnp.bfloat16).reshape(rows, parts, local_width).transpose(1, 0, 2)
    pieces = lax.all_to_all(pieces, "tp", 0, 0, tiled=True)
    mine = jnp.sum(pieces.astype(jnp.float32), axis=0)
    return (tier_source_concatenated.astype(jnp.float32) + mine).astype(jnp.bfloat16)


def solution(mesh):
    groups = 8 if mesh.shape["seq"] % 8 == 0 else 1
    devices = mesh.devices.reshape(mesh.shape["seq"] // groups, groups, mesh.shape["tp"])
    mesh = jax.sharding.Mesh(devices, ("seq_hi", "seq_lo", "tp"))
    in_specs = (
        P(SEQ, "tp"),
        P(),
        P(),
        P(),
        P(),
        P(None, None, "tp"),
        P(),
        P(None, "tp"),
        P("tp"),
        P("tp"),
        P("tp"),
        P("tp"),
        P("tp", None),
    )
    out_specs = P(SEQ, "tp")
    return jax.shard_map(body, mesh=mesh, in_specs=in_specs, out_specs=out_specs, check_vma=False)
```

```python
import math

import jax
import jax.numpy as jnp
from jax import lax
from jax.sharding import PartitionSpec as P

CHANNELS_ONE_HEAD = 64


highest = lax.Precision.HIGHEST


SEQ = ("seq_hi", "seq_lo")


def size_of(axes):
    return math.prod(lax.axis_size(axis) for axis in axes)


def from_behind(block, axis, distance):
    devices = range(size_of(axis))
    route = [(i - distance, i) for i in devices if i - distance in devices]
    return lax.ppermute(block, axis, route)


def layer_norm(rows, gain, bias, eps):
    mean = jnp.mean(rows, axis=-1, keepdims=True)
    centred = rows - mean
    spread = jnp.mean(centred * centred, axis=-1, keepdims=True)
    return centred * lax.rsqrt(spread + eps) * gain + bias


def body(
    tier_source_concatenated,
    prompt_sizes_ordered,
    tier_standardize_scale,
    tier_standardize_offset,
    previous_item_mixers,
    mapping_matrices_pile,
    fading_narrow_left,
    fading_narrow_right,
    feature_fading_baseline,
    diagonal_boost_coefficient,
    cluster_standardize_scale,
    cluster_standardize_offset,
    emitted_mapping_matrix,
):
    rows = tier_source_concatenated.shape[0]
    local_width = mapping_matrices_pile.shape[2]
    mixing_values_divided = local_width // CHANNELS_ONE_HEAD
    block = min(32, rows)
    blocks = rows // block
    full = lax.all_gather(tier_source_concatenated, "tp", axis=1, tiled=True)
    normed = layer_norm(
        full.astype(jnp.float32), tier_standardize_scale, tier_standardize_offset, 1e-05
    ).astype(jnp.bfloat16)
    first = jnp.cumsum(prompt_sizes_ordered) - prompt_sizes_ordered
    position = lax.axis_index(SEQ) * rows + jnp.arange(rows, dtype=jnp.int32)
    is_start = jnp.any(position[:, None] == first[None, :], axis=1)
    segment = jnp.sum((first[None, :] <= position[:, None]).astype(jnp.int32), axis=1)
    def blend(previous, rows_normed):
        base = rows_normed.astype(jnp.float32)
        delta = previous.astype(jnp.float32) - base
        return (base[None] + delta[None] * previous_item_mixers[:, None, :]).astype(jnp.bfloat16)

    def project(mixed):
        return (
            jnp.einsum(
                "itd,ide->ite", mixed[:4], mapping_matrices_pile, preferred_element_type=jnp.float32
            ),
            jnp.dot(mixed[4], fading_narrow_left, preferred_element_type=jnp.float32),
        )

    previous = jnp.concatenate([jnp.zeros_like(normed[:1]), normed[: rows - 1]], axis=0)
    previous = jnp.where(is_start[:, None], jnp.zeros_like(previous), previous)
    projected, lowrank = project(blend(previous, normed))
    edge = from_behind(normed[rows - 1 :], SEQ, 1)
    edge = jnp.where(is_start[0], jnp.zeros_like(edge), edge)
    edge_mixed = blend(edge, normed[:1])
    edge_pair = jnp.einsum(
        "itd,ide->ite", edge_mixed[1:3], mapping_matrices_pile[1:3], preferred_element_type=jnp.float32
    )
    key_rows = lax.dynamic_update_slice(projected[1], edge_pair[0], (0, 0)).astype(jnp.bfloat16)
    value_rows = lax.dynamic_update_slice(projected[2], edge_pair[1], (0, 0)).astype(jnp.bfloat16)
    edge_lowrank = jnp.dot(edge_mixed[4], fading_narrow_left, preferred_element_type=jnp.float32)
    lowrank = lax.dynamic_update_slice(lowrank, edge_lowrank, (0, 0))

    def late_rows(projected, edge_mixed, index):
        edge_row = jnp.dot(edge_mixed[index], mapping_matrices_pile[index], preferred_element_type=jnp.float32)
        return lax.dynamic_update_slice(projected[index], edge_row, (0, 0))
    lowrank_decay_delta = jnp.tanh(lowrank).astype(jnp.bfloat16)
    decay_logarithm = -feature_fading_baseline[None, :] * jnp.exp(
        jnp.dot(lowrank_decay_delta, fading_narrow_right, preferred_element_type=jnp.float32)
    )

    def split_heads(values):
        return (
            values.astype(jnp.float32)
            .reshape(blocks, block, mixing_values_divided, CHANNELS_ONE_HEAD)
            .transpose(0, 2, 1, 3)
        )

    inputs = (
        split_heads(key_rows),
        split_heads(value_rows),
        split_heads(decay_logarithm),
        segment.reshape(blocks, block),
        is_start.astype(jnp.float32).reshape(blocks, block),
    )
    order = jnp.arange(block)
    lower_incl = (order[None, :] <= order[:, None]).astype(jnp.float32)
    strictly = order[None, :] < order[:, None]
    diagonal_extra_contribution = diagonal_boost_coefficient.reshape(
        mixing_values_divided, CHANNELS_ONE_HEAD
    )

    query_array_tile, content_slab, lw_b, seg_b, start_b = inputs
    incl = jnp.einsum("ts,bhsc->bhtc", lower_incl, lw_b, precision=highest)
    excl = incl - lw_b
    seen = jnp.einsum("ts,bs->bt", lower_incl, start_b, precision=highest)
    valid = (seen == 0.0).astype(jnp.float32)
    decay_factor = jnp.exp(excl) * valid[:, None, :, None]
    total = incl[:, :, block - 1, :]
    keep = (seen[:, block - 1] == 0.0).astype(jnp.float32)
    tail_ok = (seg_b == seg_b[:, block - 1 :]).astype(jnp.float32)
    tail = query_array_tile * jnp.exp(total[:, :, None, :] - incl) * tail_ok[:, None, :, None]
    block_state = jnp.einsum("bhsc,bhsv->bhcv", tail, content_slab, precision=highest)
    block_decay = keep[:, None, None] * jnp.exp(total)

    state = jnp.zeros_like(block_state[0])
    offset = jnp.zeros_like(total[0])
    alive = jnp.float32(1.0)
    entering, reach = [], []
    for index in range(blocks):
        entering.append(state)
        reach.append(alive * jnp.exp(offset))
        state = block_decay[index][:, :, None] * state + block_state[index]
        offset = offset + total[index]
        alive = alive * keep[index]
    entering = jnp.stack(entering)
    reach = jnp.stack(reach)[:, :, None, :]
    end_state = state
    decay_total = alive * jnp.exp(offset)

    packed = jnp.concatenate([end_state, decay_total[:, None, :]], axis=1)

    def combine(received, own):
        own_state, own_decay = own[:, :CHANNELS_ONE_HEAD], own[:, CHANNELS_ONE_HEAD:]
        got_state, got_decay = received[:, :CHANNELS_ONE_HEAD], received[:, CHANNELS_ONE_HEAD:]
        state = jnp.transpose(own_decay, (0, 2, 1)) * got_state + own_state
        return jnp.concatenate([state, own_decay * got_decay], axis=1)

    devices = size_of(SEQ)
    def block_scores(index, incl_b, excl_b, recept_b, key_b):
        pair_ok = strictly & (seg_b[index][None, :] == seg_b[index][:, None])
        gap = jnp.minimum(excl_b[:, :, None, :] - incl_b[:, None, :, :], 0.0)
        weight = jnp.where(pair_ok[None, :, :, None], jnp.exp(gap), 0.0)
        return jnp.einsum("htc,hsc,htsc->hts", recept_b, key_b, weight, precision=highest)

    scores = []
    prefix = from_behind(packed, SEQ, 1)
    prefix, late = lax.optimization_barrier((prefix, (projected, edge_mixed)))
    recept = late_rows(*late, 0).astype(jnp.bfloat16)
    gate = jax.nn.silu(late_rows(*late, 3)).astype(jnp.bfloat16)
    gating_rows_tile = split_heads(recept)
    carried = gating_rows_tile * decay_factor
    from_start = carried * reach
    present_item_reward = jnp.sum(
        gating_rows_tile * diagonal_extra_contribution[None, :, None, :] * query_array_tile, axis=-1
    )
    distance = 1
    while distance < devices:
        prefix = combine(from_behind(prefix, SEQ, distance), prefix)
        distance *= 2
        index = len(scores)
        if index < blocks:
            operands = (incl[index], excl[index], gating_rows_tile[index], query_array_tile[index])
            prefix, operands = lax.optimization_barrier((prefix, operands))
            scores.append(block_scores(index, *operands))
    for index in range(len(scores), blocks):
        scores.append(
            block_scores(index, incl[index], excl[index], gating_rows_tile[index], query_array_tile[index])
        )
    scores = jnp.stack(scores)
    outs = (
        jnp.einsum("bhts,bhsv->bhtv", scores, content_slab, precision=highest)
        + present_item_reward[..., None] * content_slab
        + jnp.einsum("bhtc,bhcv->bhtv", carried, entering, precision=highest)
    )
    incoming = prefix[:, :CHANNELS_ONE_HEAD]
    outs = outs + jnp.einsum("bhtc,hcv->bhtv", from_start, incoming, precision=highest)
    wkv = outs.transpose(0, 2, 1, 3).reshape(rows, mixing_values_divided, CHANNELS_ONE_HEAD)
    mean = jnp.mean(wkv, axis=-1, keepdims=True)
    centred = wkv - mean
    spread = jnp.mean(centred * centred, axis=-1, keepdims=True)
    grouped = (centred * lax.rsqrt(spread + 0.00064)).reshape(
        rows, local_width
    ) * cluster_standardize_scale + cluster_standardize_offset
    gated = (grouped * gate.astype(jnp.float32)).astype(jnp.bfloat16)
    partial_sum = jnp.dot(gated, emitted_mapping_matrix, preferred_element_type=jnp.float32)
    parts = lax.axis_size("tp")
    pieces = partial_sum.astype(jnp.bfloat16).reshape(rows, parts, local_width).transpose(1, 0, 2)
    pieces = lax.all_to_all(pieces, "tp", 0, 0, tiled=True)
    mine = jnp.sum(pieces.astype(jnp.float32), axis=0)
    return (tier_source_concatenated.astype(jnp.float32) + mine).astype(jnp.bfloat16)


def solution(mesh):
    groups = 8 if mesh.shape["seq"] % 8 == 0 else 1
    devices = mesh.devices.reshape(mesh.shape["seq"] // groups, groups, mesh.shape["tp"])
    mesh = jax.sharding.Mesh(devices, ("seq_hi", "seq_lo", "tp"))
    in_specs = (
        P(SEQ, "tp"),
        P(),
        P(),
        P(),
        P(),
        P(None, None, "tp"),
        P(),
        P(None, "tp"),
        P("tp"),
        P("tp"),
        P("tp"),
        P("tp"),
        P("tp", None),
    )
    out_specs = P(SEQ, "tp")
    return jax.shard_map(body, mesh=mesh, in_specs=in_specs, out_specs=out_specs, check_vma=False)
```

```python
import math

import jax
import jax.numpy as jnp
from jax import lax
from jax.sharding import PartitionSpec as P

CHANNELS_ONE_HEAD = 64


highest = lax.Precision.HIGHEST


SEQ = ("seq_hi", "seq_lo")


def size_of(axes):
    return math.prod(lax.axis_size(axis) for axis in axes)


def from_behind(block, axis, distance):
    devices = range(size_of(axis))
    route = [(i - distance, i) for i in devices if i - distance in devices]
    return lax.ppermute(block, axis, route)


def layer_norm(rows, gain, bias, eps):
    mean = jnp.mean(rows, axis=-1, keepdims=True)
    centred = rows - mean
    spread = jnp.mean(centred * centred, axis=-1, keepdims=True)
    return centred * lax.rsqrt(spread + eps) * gain + bias


def body(
    tier_source_concatenated,
    prompt_sizes_ordered,
    tier_standardize_scale,
    tier_standardize_offset,
    previous_item_mixers,
    mapping_matrices_pile,
    fading_narrow_left,
    fading_narrow_right,
    feature_fading_baseline,
    diagonal_boost_coefficient,
    cluster_standardize_scale,
    cluster_standardize_offset,
    emitted_mapping_matrix,
):
    rows = tier_source_concatenated.shape[0]
    local_width = mapping_matrices_pile.shape[2]
    mixing_values_divided = local_width // CHANNELS_ONE_HEAD
    block = min(32, rows)
    blocks = rows // block
    full = lax.all_gather(tier_source_concatenated, "tp", axis=1, tiled=True)
    normed = layer_norm(
        full.astype(jnp.float32), tier_standardize_scale, tier_standardize_offset, 1e-05
    ).astype(jnp.bfloat16)
    first = jnp.cumsum(prompt_sizes_ordered) - prompt_sizes_ordered
    position = lax.axis_index(SEQ) * rows + jnp.arange(rows, dtype=jnp.int32)
    is_start = jnp.any(position[:, None] == first[None, :], axis=1)
    segment = jnp.sum((first[None, :] <= position[:, None]).astype(jnp.int32), axis=1)
    def blend(previous, rows_normed):
        base = rows_normed.astype(jnp.float32)
        delta = previous.astype(jnp.float32) - base
        return (base[None] + delta[None] * previous_item_mixers[:, None, :]).astype(jnp.bfloat16)

    def project(mixed):
        return (
            jnp.einsum(
                "itd,ide->ite", mixed[:4], mapping_matrices_pile, preferred_element_type=jnp.float32
            ),
            jnp.dot(mixed[4], fading_narrow_left, preferred_element_type=jnp.float32),
        )

    previous = jnp.concatenate([jnp.zeros_like(normed[:1]), normed[: rows - 1]], axis=0)
    previous = jnp.where(is_start[:, None], jnp.zeros_like(previous), previous)
    projected, lowrank = project(blend(previous, normed))
    edge = from_behind(normed[rows - 1 :], SEQ, 1)
    edge = jnp.where(is_start[0], jnp.zeros_like(edge), edge)
    edge_projected, edge_lowrank = project(blend(edge, normed[:1]))
    projected = lax.dynamic_update_slice(projected, edge_projected, (0, 0, 0))
    lowrank = lax.dynamic_update_slice(lowrank, edge_lowrank, (0, 0))
    recept = projected[0].astype(jnp.bfloat16)
    key_rows = projected[1].astype(jnp.bfloat16)
    value_rows = projected[2].astype(jnp.bfloat16)
    gate = jax.nn.silu(projected[3]).astype(jnp.bfloat16)
    lowrank_decay_delta = jnp.tanh(lowrank).astype(jnp.bfloat16)
    decay_logarithm = -feature_fading_baseline[None, :] * jnp.exp(
        jnp.dot(lowrank_decay_delta, fading_narrow_right, preferred_element_type=jnp.float32)
    )

    def split_heads(values):
        return (
            values.astype(jnp.float32)
            .reshape(blocks, block, mixing_values_divided, CHANNELS_ONE_HEAD)
            .transpose(0, 2, 1, 3)
        )

    inputs = (
        split_heads(recept),
        split_heads(key_rows),
        split_heads(value_rows),
        split_heads(decay_logarithm),
        segment.reshape(blocks, block),
        is_start.astype(jnp.float32).reshape(blocks, block),
    )
    order = jnp.arange(block)
    lower_incl = (order[None, :] <= order[:, None]).astype(jnp.float32)
    strictly = order[None, :] < order[:, None]
    diagonal_extra_contribution = diagonal_boost_coefficient.reshape(
        mixing_values_divided, CHANNELS_ONE_HEAD
    )

    gating_rows_tile, query_array_tile, content_slab, lw_b, seg_b, start_b = inputs
    incl = jnp.einsum("ts,bhsc->bhtc", lower_incl, lw_b, precision=highest)
    excl = incl - lw_b
    present_item_reward = jnp.sum(
        gating_rows_tile * diagonal_extra_contribution[None, :, None, :] * query_array_tile, axis=-1
    )
    seen = jnp.einsum("ts,bs->bt", lower_incl, start_b, precision=highest)
    valid = (seen == 0.0).astype(jnp.float32)
    carried = gating_rows_tile * jnp.exp(excl) * valid[:, None, :, None]
    total = incl[:, :, block - 1, :]
    keep = (seen[:, block - 1] == 0.0).astype(jnp.float32)
    tail_ok = (seg_b == seg_b[:, block - 1 :]).astype(jnp.float32)
    tail = query_array_tile * jnp.exp(total[:, :, None, :] - incl) * tail_ok[:, None, :, None]
    block_state = jnp.einsum("bhsc,bhsv->bhcv", tail, content_slab, precision=highest)
    block_decay = keep[:, None, None] * jnp.exp(total)

    state = jnp.zeros_like(block_state[0])
    offset = jnp.zeros_like(total[0])
    alive = jnp.float32(1.0)
    entering, reach = [], []
    for index in range(blocks):
        entering.append(state)
        reach.append(alive * jnp.exp(offset))
        state = block_decay[index][:, :, None] * state + block_state[index]
        offset = offset + total[index]
        alive = alive * keep[index]
    entering = jnp.stack(entering)
    from_start = carried * jnp.stack(reach)[:, :, None, :]
    end_state = state
    decay_total = alive * jnp.exp(offset)

    packed = jnp.concatenate([end_state, decay_total[:, None, :]], axis=1)

    def combine(received, own):
        own_state, own_decay = own[:, :CHANNELS_ONE_HEAD], own[:, CHANNELS_ONE_HEAD:]
        got_state, got_decay = received[:, :CHANNELS_ONE_HEAD], received[:, CHANNELS_ONE_HEAD:]
        state = jnp.transpose(own_decay, (0, 2, 1)) * got_state + own_state
        return jnp.concatenate([state, own_decay * got_decay], axis=1)

    devices = size_of(SEQ)
    def block_scores(index, incl_b, excl_b, recept_b, key_b):
        pair_ok = strictly & (seg_b[index][None, :] == seg_b[index][:, None])
        gap = jnp.minimum(excl_b[:, :, None, :] - incl_b[:, None, :, :], 0.0)
        weight = jnp.where(pair_ok[None, :, :, None], jnp.exp(gap), 0.0)
        scores = jnp.einsum("htc,hsc,htsc->hts", recept_b, key_b, weight, precision=highest)
        return jnp.einsum("hts,hsv->htv", scores, content_slab[index], precision=highest)

    scores = []
    prefix = from_behind(packed, SEQ, 1)
    distance = 1
    while distance < devices:
        prefix = combine(from_behind(prefix, SEQ, distance), prefix)
        distance *= 2
        index = len(scores)
        if index < blocks:
            operands = (incl[index], excl[index], gating_rows_tile[index], query_array_tile[index])
            prefix, operands = lax.optimization_barrier((prefix, operands))
            scores.append(block_scores(index, *operands))
    for index in range(len(scores), blocks):
        scores.append(
            block_scores(index, incl[index], excl[index], gating_rows_tile[index], query_array_tile[index])
        )
    outs = (
        jnp.stack(scores)
        + present_item_reward[..., None] * content_slab
        + jnp.einsum("bhtc,bhcv->bhtv", carried, entering, precision=highest)
    )
    incoming = prefix[:, :CHANNELS_ONE_HEAD]
    outs = outs + jnp.einsum("bhtc,hcv->bhtv", from_start, incoming, precision=highest)
    wkv = outs.transpose(0, 2, 1, 3).reshape(rows, mixing_values_divided, CHANNELS_ONE_HEAD)
    mean = jnp.mean(wkv, axis=-1, keepdims=True)
    centred = wkv - mean
    spread = jnp.mean(centred * centred, axis=-1, keepdims=True)
    grouped = (centred * lax.rsqrt(spread + 0.00064)).reshape(
        rows, local_width
    ) * cluster_standardize_scale + cluster_standardize_offset
    gated = (grouped * gate.astype(jnp.float32)).astype(jnp.bfloat16)
    partial_sum = jnp.dot(gated, emitted_mapping_matrix, preferred_element_type=jnp.float32)
    parts = lax.axis_size("tp")
    pieces = partial_sum.astype(jnp.bfloat16).reshape(rows, parts, local_width).transpose(1, 0, 2)
    pieces = lax.all_to_all(pieces, "tp", 0, 0, tiled=True)
    mine = jnp.sum(pieces.astype(jnp.float32), axis=0)
    return (tier_source_concatenated.astype(jnp.float32) + mine).astype(jnp.bfloat16)


def solution(mesh):
    groups = 8 if mesh.shape["seq"] % 8 == 0 else 1
    devices = mesh.devices.reshape(mesh.shape["seq"] // groups, groups, mesh.shape["tp"])
    mesh = jax.sharding.Mesh(devices, ("seq_hi", "seq_lo", "tp"))
    in_specs = (
        P(SEQ, "tp"),
        P(),
        P(),
        P(),
        P(),
        P(None, None, "tp"),
        P(),
        P(None, "tp"),
        P("tp"),
        P("tp"),
        P("tp"),
        P("tp"),
        P("tp", None),
    )
    out_specs = P(SEQ, "tp")
    return jax.shard_map(body, mesh=mesh, in_specs=in_specs, out_specs=out_specs, check_vma=False)
```

```python
import math

import jax
import jax.numpy as jnp
from jax import lax
from jax.sharding import PartitionSpec as P

CHANNELS_ONE_HEAD = 64


highest = lax.Precision.HIGHEST


SEQ = ("seq_hi", "seq_lo")


def size_of(axes):
    return math.prod(lax.axis_size(axis) for axis in axes)


def from_behind(block, axis, distance):
    devices = range(size_of(axis))
    route = [(i - distance, i) for i in devices if i - distance in devices]
    return lax.ppermute(block, axis, route)


def layer_norm(rows, gain, bias, eps):
    mean = jnp.mean(rows, axis=-1, keepdims=True)
    centred = rows - mean
    spread = jnp.mean(centred * centred, axis=-1, keepdims=True)
    return centred * lax.rsqrt(spread + eps) * gain + bias


def body(
    tier_source_concatenated,
    prompt_sizes_ordered,
    tier_standardize_scale,
    tier_standardize_offset,
    previous_item_mixers,
    mapping_matrices_pile,
    fading_narrow_left,
    fading_narrow_right,
    feature_fading_baseline,
    diagonal_boost_coefficient,
    cluster_standardize_scale,
    cluster_standardize_offset,
    emitted_mapping_matrix,
):
    rows = tier_source_concatenated.shape[0]
    local_width = mapping_matrices_pile.shape[2]
    mixing_values_divided = local_width // CHANNELS_ONE_HEAD
    block = min(16, rows)
    blocks = rows // block
    full = lax.all_gather(tier_source_concatenated, "tp", axis=1, tiled=True)
    normed = layer_norm(
        full.astype(jnp.float32), tier_standardize_scale, tier_standardize_offset, 1e-05
    ).astype(jnp.bfloat16)
    first = jnp.cumsum(prompt_sizes_ordered) - prompt_sizes_ordered
    position = lax.axis_index(SEQ) * rows + jnp.arange(rows, dtype=jnp.int32)
    is_start = jnp.any(position[:, None] == first[None, :], axis=1)
    segment = jnp.sum((first[None, :] <= position[:, None]).astype(jnp.int32), axis=1)
    def blend(previous, rows_normed):
        base = rows_normed.astype(jnp.float32)
        delta = previous.astype(jnp.float32) - base
        return (base[None] + delta[None] * previous_item_mixers[:, None, :]).astype(jnp.bfloat16)

    def project(mixed):
        return (
            jnp.einsum(
                "itd,ide->ite", mixed[:4], mapping_matrices_pile, preferred_element_type=jnp.float32
            ),
            jnp.dot(mixed[4], fading_narrow_left, preferred_element_type=jnp.float32),
        )

    previous = jnp.concatenate([jnp.zeros_like(normed[:1]), normed[: rows - 1]], axis=0)
    previous = jnp.where(is_start[:, None], jnp.zeros_like(previous), previous)
    projected, lowrank = project(blend(previous, normed))
    edge = from_behind(normed[rows - 1 :], SEQ, 1)
    edge = jnp.where(is_start[0], jnp.zeros_like(edge), edge)
    edge_projected, edge_lowrank = project(blend(edge, normed[:1]))
    projected = lax.dynamic_update_slice(projected, edge_projected, (0, 0, 0))
    lowrank = lax.dynamic_update_slice(lowrank, edge_lowrank, (0, 0))
    recept = projected[0].astype(jnp.bfloat16)
    key_rows = projected[1].astype(jnp.bfloat16)
    value_rows = projected[2].astype(jnp.bfloat16)
    gate = jax.nn.silu(projected[3]).astype(jnp.bfloat16)
    lowrank_decay_delta = jnp.tanh(lowrank).astype(jnp.bfloat16)
    decay_logarithm = -feature_fading_baseline[None, :] * jnp.exp(
        jnp.dot(lowrank_decay_delta, fading_narrow_right, preferred_element_type=jnp.float32)
    )

    def split_heads(values):
        return (
            values.astype(jnp.float32)
            .reshape(blocks, block, mixing_values_divided, CHANNELS_ONE_HEAD)
            .transpose(0, 2, 1, 3)
        )

    inputs = (
        split_heads(recept),
        split_heads(key_rows),
        split_heads(value_rows),
        split_heads(decay_logarithm),
        segment.reshape(blocks, block),
        is_start.astype(jnp.float32).reshape(blocks, block),
    )
    order = jnp.arange(block)
    lower_incl = (order[None, :] <= order[:, None]).astype(jnp.float32)
    strictly = order[None, :] < order[:, None]
    diagonal_extra_contribution = diagonal_boost_coefficient.reshape(
        mixing_values_divided, CHANNELS_ONE_HEAD
    )

    gating_rows_tile, query_array_tile, content_slab, lw_b, seg_b, start_b = inputs
    incl = jnp.einsum("ts,bhsc->bhtc", lower_incl, lw_b, precision=highest)
    excl = incl - lw_b
    present_item_reward = jnp.sum(
        gating_rows_tile * diagonal_extra_contribution[None, :, None, :] * query_array_tile, axis=-1
    )
    seen = jnp.einsum("ts,bs->bt", lower_incl, start_b, precision=highest)
    valid = (seen == 0.0).astype(jnp.float32)
    carried = gating_rows_tile * jnp.exp(excl) * valid[:, None, :, None]
    total = incl[:, :, block - 1, :]
    keep = (seen[:, block - 1] == 0.0).astype(jnp.float32)
    tail_ok = (seg_b == seg_b[:, block - 1 :]).astype(jnp.float32)
    tail = query_array_tile * jnp.exp(total[:, :, None, :] - incl) * tail_ok[:, None, :, None]
    block_state = jnp.einsum("bhsc,bhsv->bhcv", tail, content_slab, precision=highest)
    block_decay = keep[:, None, None] * jnp.exp(total)

    state = jnp.zeros_like(block_state[0])
    offset = jnp.zeros_like(total[0])
    alive = jnp.float32(1.0)
    entering, reach = [], []
    for index in range(blocks):
        entering.append(state)
        reach.append(alive * jnp.exp(offset))
        state = block_decay[index][:, :, None] * state + block_state[index]
        offset = offset + total[index]
        alive = alive * keep[index]
    entering = jnp.stack(entering)
    from_start = carried * jnp.stack(reach)[:, :, None, :]
    end_state = state
    decay_total = alive * jnp.exp(offset)

    packed = jnp.concatenate([end_state, decay_total[:, None, :]], axis=1)

    def combine(received, own):
        own_state, own_decay = own[:, :CHANNELS_ONE_HEAD], own[:, CHANNELS_ONE_HEAD:]
        got_state, got_decay = received[:, :CHANNELS_ONE_HEAD], received[:, CHANNELS_ONE_HEAD:]
        state = jnp.transpose(own_decay, (0, 2, 1)) * got_state + own_state
        return jnp.concatenate([state, own_decay * got_decay], axis=1)

    devices = size_of(SEQ)
    def block_scores(seg_g, incl_g, excl_g, recept_g, key_g):
        pair_ok = strictly[None] & (seg_g[:, None, :] == seg_g[:, :, None])
        gap = jnp.minimum(excl_g[:, :, :, None, :] - incl_g[:, :, None, :, :], 0.0)
        weight = jnp.where(pair_ok[:, None, :, :, None], jnp.exp(gap), 0.0)
        return jnp.einsum("bhtc,bhsc,bhtsc->bhts", recept_g, key_g, weight, precision=highest)

    group = max(1, blocks // 4)
    groups = blocks // group

    def group_operands(index):
        part = slice(index * group, (index + 1) * group)
        return (incl[part], excl[part], gating_rows_tile[part], query_array_tile[part])

    scores = []
    prefix = from_behind(packed, SEQ, 1)
    distance = 1
    while distance < devices:
        prefix = combine(from_behind(prefix, SEQ, distance), prefix)
        distance *= 2
        index = len(scores)
        if index < groups:
            prefix, operands = lax.optimization_barrier((prefix, group_operands(index)))
            scores.append(block_scores(seg_b[index * group : (index + 1) * group], *operands))
    for index in range(len(scores), groups):
        scores.append(block_scores(seg_b[index * group : (index + 1) * group], *group_operands(index)))
    scores = jnp.concatenate(scores, axis=0)
    outs = (
        jnp.einsum("bhts,bhsv->bhtv", scores, content_slab, precision=highest)
        + present_item_reward[..., None] * content_slab
        + jnp.einsum("bhtc,bhcv->bhtv", carried, entering, precision=highest)
    )
    incoming = prefix[:, :CHANNELS_ONE_HEAD]
    outs = outs + jnp.einsum("bhtc,hcv->bhtv", from_start, incoming, precision=highest)
    wkv = outs.transpose(0, 2, 1, 3).reshape(rows, mixing_values_divided, CHANNELS_ONE_HEAD)
    mean = jnp.mean(wkv, axis=-1, keepdims=True)
    centred = wkv - mean
    spread = jnp.mean(centred * centred, axis=-1, keepdims=True)
    grouped = (centred * lax.rsqrt(spread + 0.00064)).reshape(
        rows, local_width
    ) * cluster_standardize_scale + cluster_standardize_offset
    gated = (grouped * gate.astype(jnp.float32)).astype(jnp.bfloat16)
    partial_sum = jnp.dot(gated, emitted_mapping_matrix, preferred_element_type=jnp.float32)
    parts = lax.axis_size("tp")
    pieces = partial_sum.astype(jnp.bfloat16).reshape(rows, parts, local_width).transpose(1, 0, 2)
    pieces = lax.all_to_all(pieces, "tp", 0, 0, tiled=True)
    mine = jnp.sum(pieces.astype(jnp.float32), axis=0)
    return (tier_source_concatenated.astype(jnp.float32) + mine).astype(jnp.bfloat16)


def solution(mesh):
    groups = 8 if mesh.shape["seq"] % 8 == 0 else 1
    devices = mesh.devices.reshape(mesh.shape["seq"] // groups, groups, mesh.shape["tp"])
    mesh = jax.sharding.Mesh(devices, ("seq_hi", "seq_lo", "tp"))
    in_specs = (
        P(SEQ, "tp"),
        P(),
        P(),
        P(),
        P(),
        P(None, None, "tp"),
        P(),
        P(None, "tp"),
        P("tp"),
        P("tp"),
        P("tp"),
        P("tp"),
        P("tp", None),
    )
    out_specs = P(SEQ, "tp")
    return jax.shard_map(body, mesh=mesh, in_specs=in_specs, out_specs=out_specs, check_vma=False)
```

```python
import math

import jax
import jax.numpy as jnp
from jax import lax
from jax.sharding import PartitionSpec as P

CHANNELS_ONE_HEAD = 64


highest = lax.Precision.HIGHEST


SEQ = ("seq_hi", "seq_lo")


def size_of(axes):
    return math.prod(lax.axis_size(axis) for axis in axes)


def from_behind(block, axis, distance):
    devices = range(size_of(axis))
    route = [(i - distance, i) for i in devices if i - distance in devices]
    return lax.ppermute(block, axis, route)


def layer_norm(rows, gain, bias, eps):
    mean = jnp.mean(rows, axis=-1, keepdims=True)
    centred = rows - mean
    spread = jnp.mean(centred * centred, axis=-1, keepdims=True)
    return centred * lax.rsqrt(spread + eps) * gain + bias


def body(
    tier_source_concatenated,
    prompt_sizes_ordered,
    tier_standardize_scale,
    tier_standardize_offset,
    previous_item_mixers,
    mapping_matrices_pile,
    fading_narrow_left,
    fading_narrow_right,
    feature_fading_baseline,
    diagonal_boost_coefficient,
    cluster_standardize_scale,
    cluster_standardize_offset,
    emitted_mapping_matrix,
):
    rows = tier_source_concatenated.shape[0]
    local_width = mapping_matrices_pile.shape[2]
    mixing_values_divided = local_width // CHANNELS_ONE_HEAD
    block = min(32, rows)
    blocks = rows // block
    parts = lax.axis_size("tp")
    copies = jnp.broadcast_to(tier_source_concatenated[None], (parts,) + tier_source_concatenated.shape)
    full = lax.all_to_all(copies, "tp", 0, 0, tiled=True).transpose(1, 0, 2).reshape(rows, -1)
    normed = layer_norm(
        full.astype(jnp.float32), tier_standardize_scale, tier_standardize_offset, 1e-05
    ).astype(jnp.bfloat16)
    first = jnp.cumsum(prompt_sizes_ordered) - prompt_sizes_ordered
    position = lax.axis_index(SEQ) * rows + jnp.arange(rows, dtype=jnp.int32)
    is_start = jnp.any(position[:, None] == first[None, :], axis=1)
    segment = jnp.sum((first[None, :] <= position[:, None]).astype(jnp.int32), axis=1)
    def blend(previous, rows_normed):
        base = rows_normed.astype(jnp.float32)
        delta = previous.astype(jnp.float32) - base
        return (base[None] + delta[None] * previous_item_mixers[:, None, :]).astype(jnp.bfloat16)

    def project(mixed):
        return (
            jnp.einsum(
                "itd,ide->ite", mixed[:4], mapping_matrices_pile, preferred_element_type=jnp.float32
            ),
            jnp.dot(mixed[4], fading_narrow_left, preferred_element_type=jnp.float32),
        )

    previous = jnp.concatenate([jnp.zeros_like(normed[:1]), normed[: rows - 1]], axis=0)
    previous = jnp.where(is_start[:, None], jnp.zeros_like(previous), previous)
    projected, lowrank = project(blend(previous, normed))
    edge = from_behind(normed[rows - 1 :], SEQ, 1)
    edge = jnp.where(is_start[0], jnp.zeros_like(edge), edge)
    edge_projected, edge_lowrank = project(blend(edge, normed[:1]))
    projected = lax.dynamic_update_slice(projected, edge_projected, (0, 0, 0))
    lowrank = lax.dynamic_update_slice(lowrank, edge_lowrank, (0, 0))
    recept = projected[0].astype(jnp.bfloat16)
    key_rows = projected[1].astype(jnp.bfloat16)
    value_rows = projected[2].astype(jnp.bfloat16)
    gate = jax.nn.silu(projected[3]).astype(jnp.bfloat16)
    lowrank_decay_delta = jnp.tanh(lowrank).astype(jnp.bfloat16)
    decay_logarithm = -feature_fading_baseline[None, :] * jnp.exp(
        jnp.dot(lowrank_decay_delta, fading_narrow_right, preferred_element_type=jnp.float32)
    )

    def split_heads(values):
        return (
            values.astype(jnp.float32)
            .reshape(blocks, block, mixing_values_divided, CHANNELS_ONE_HEAD)
            .transpose(0, 2, 1, 3)
        )

    inputs = (
        split_heads(recept),
        split_heads(key_rows),
        split_heads(value_rows),
        split_heads(decay_logarithm),
        segment.reshape(blocks, block),
        is_start.astype(jnp.float32).reshape(blocks, block),
    )
    order = jnp.arange(block)
    lower_incl = (order[None, :] <= order[:, None]).astype(jnp.float32)
    strictly = order[None, :] < order[:, None]
    diagonal_extra_contribution = diagonal_boost_coefficient.reshape(
        mixing_values_divided, CHANNELS_ONE_HEAD
    )

    gating_rows_tile, query_array_tile, content_slab, lw_b, seg_b, start_b = inputs
    incl = jnp.einsum("ts,bhsc->bhtc", lower_incl, lw_b, precision=highest)
    excl = incl - lw_b
    present_item_reward = jnp.sum(
        gating_rows_tile * diagonal_extra_contribution[None, :, None, :] * query_array_tile, axis=-1
    )
    seen = jnp.einsum("ts,bs->bt", lower_incl, start_b, precision=highest)
    valid = (seen == 0.0).astype(jnp.float32)
    carried = gating_rows_tile * jnp.exp(excl) * valid[:, None, :, None]
    total = incl[:, :, block - 1, :]
    keep = (seen[:, block - 1] == 0.0).astype(jnp.float32)
    tail_ok = (seg_b == seg_b[:, block - 1 :]).astype(jnp.float32)
    tail = query_array_tile * jnp.exp(total[:, :, None, :] - incl) * tail_ok[:, None, :, None]
    block_state = jnp.einsum("bhsc,bhsv->bhcv", tail, content_slab, precision=highest)
    block_decay = keep[:, None, None] * jnp.exp(total)

    state = jnp.zeros_like(block_state[0])
    offset = jnp.zeros_like(total[0])
    alive = jnp.float32(1.0)
    entering, reach = [], []
    for index in range(blocks):
        entering.append(state)
        reach.append(alive * jnp.exp(offset))
        state = block_decay[index][:, :, None] * state + block_state[index]
        offset = offset + total[index]
        alive = alive * keep[index]
    entering = jnp.stack(entering)
    from_start = carried * jnp.stack(reach)[:, :, None, :]
    end_state = state
    decay_total = alive * jnp.exp(offset)

    packed = jnp.concatenate([end_state, decay_total[:, None, :]], axis=1)

    def combine(received, own):
        own_state, own_decay = own[:, :CHANNELS_ONE_HEAD], own[:, CHANNELS_ONE_HEAD:]
        got_state, got_decay = received[:, :CHANNELS_ONE_HEAD], received[:, CHANNELS_ONE_HEAD:]
        state = jnp.transpose(own_decay, (0, 2, 1)) * got_state + own_state
        return jnp.concatenate([state, own_decay * got_decay], axis=1)

    devices = size_of(SEQ)
    def block_scores(index, incl_b, excl_b, recept_b, key_b):
        pair_ok = strictly & (seg_b[index][None, :] == seg_b[index][:, None])
        gap = jnp.minimum(excl_b[:, :, None, :] - incl_b[:, None, :, :], 0.0)
        weight = jnp.where(pair_ok[None, :, :, None], jnp.exp(gap), 0.0)
        return jnp.einsum("htc,hsc,htsc->hts", recept_b, key_b, weight, precision=highest)

    scores = []
    prefix = from_behind(packed, SEQ, 1)
    distance = 1
    while distance < devices:
        prefix = combine(from_behind(prefix, SEQ, distance), prefix)
        distance *= 2
        index = len(scores)
        if index < blocks:
            operands = (incl[index], excl[index], gating_rows_tile[index], query_array_tile[index])
            prefix, operands = lax.optimization_barrier((prefix, operands))
            scores.append(block_scores(index, *operands))
    for index in range(len(scores), blocks):
        scores.append(
            block_scores(index, incl[index], excl[index], gating_rows_tile[index], query_array_tile[index])
        )
    scores = jnp.stack(scores)
    outs = (
        jnp.einsum("bhts,bhsv->bhtv", scores, content_slab, precision=highest)
        + present_item_reward[..., None] * content_slab
        + jnp.einsum("bhtc,bhcv->bhtv", carried, entering, precision=highest)
    )
    incoming = prefix[:, :CHANNELS_ONE_HEAD]
    outs = outs + jnp.einsum("bhtc,hcv->bhtv", from_start, incoming, precision=highest)
    wkv = outs.transpose(0, 2, 1, 3).reshape(rows, mixing_values_divided, CHANNELS_ONE_HEAD)
    mean = jnp.mean(wkv, axis=-1, keepdims=True)
    centred = wkv - mean
    spread = jnp.mean(centred * centred, axis=-1, keepdims=True)
    grouped = (centred * lax.rsqrt(spread + 0.00064)).reshape(
        rows, local_width
    ) * cluster_standardize_scale + cluster_standardize_offset
    gated = (grouped * gate.astype(jnp.float32)).astype(jnp.bfloat16)
    partial_sum = jnp.dot(gated, emitted_mapping_matrix, preferred_element_type=jnp.float32)
    parts = lax.axis_size("tp")
    pieces = partial_sum.astype(jnp.bfloat16).reshape(rows, parts, local_width).transpose(1, 0, 2)
    pieces = lax.all_to_all(pieces, "tp", 0, 0, tiled=True)
    mine = jnp.sum(pieces.astype(jnp.float32), axis=0)
    return (tier_source_concatenated.astype(jnp.float32) + mine).astype(jnp.bfloat16)


def solution(mesh):
    groups = 8 if mesh.shape["seq"] % 8 == 0 else 1
    devices = mesh.devices.reshape(mesh.shape["seq"] // groups, groups, mesh.shape["tp"])
    mesh = jax.sharding.Mesh(devices, ("seq_hi", "seq_lo", "tp"))
    in_specs = (
        P(SEQ, "tp"),
        P(),
        P(),
        P(),
        P(),
        P(None, None, "tp"),
        P(),
        P(None, "tp"),
        P("tp"),
        P("tp"),
        P("tp"),
        P("tp"),
        P("tp", None),
    )
    out_specs = P(SEQ, "tp")
    return jax.shard_map(body, mesh=mesh, in_specs=in_specs, out_specs=out_specs, check_vma=False)
```

```python
import math

import jax
import jax.numpy as jnp
from jax import lax
from jax.sharding import PartitionSpec as P

CHANNELS_ONE_HEAD = 64


highest = lax.Precision.HIGHEST


SEQ = ("seq_hi", "seq_lo")


def size_of(axes):
    return math.prod(lax.axis_size(axis) for axis in axes)


def from_behind(block, axis, distance):
    devices = range(size_of(axis))
    route = [(i - distance, i) for i in devices if i - distance in devices]
    return lax.ppermute(block, axis, route)


def layer_norm(rows, gain, bias, eps):
    mean = jnp.mean(rows, axis=-1, keepdims=True)
    centred = rows - mean
    spread = jnp.mean(centred * centred, axis=-1, keepdims=True)
    return centred * lax.rsqrt(spread + eps) * gain + bias


def body(
    tier_source_concatenated,
    prompt_sizes_ordered,
    tier_standardize_scale,
    tier_standardize_offset,
    previous_item_mixers,
    mapping_matrices_pile,
    fading_narrow_left,
    fading_narrow_right,
    feature_fading_baseline,
    diagonal_boost_coefficient,
    cluster_standardize_scale,
    cluster_standardize_offset,
    emitted_mapping_matrix,
):
    rows = tier_source_concatenated.shape[0]
    local_width = mapping_matrices_pile.shape[2]
    mixing_values_divided = local_width // CHANNELS_ONE_HEAD
    block = min(32, rows)
    blocks = rows // block
    full = lax.all_gather(tier_source_concatenated, "tp", axis=1, tiled=True)
    normed = layer_norm(
        full.astype(jnp.float32), tier_standardize_scale, tier_standardize_offset, 1e-05
    ).astype(jnp.bfloat16)
    first = jnp.cumsum(prompt_sizes_ordered) - prompt_sizes_ordered
    position = lax.axis_index(SEQ) * rows + jnp.arange(rows, dtype=jnp.int32)
    is_start = jnp.any(position[:, None] == first[None, :], axis=1)
    segment = jnp.sum((first[None, :] <= position[:, None]).astype(jnp.int32), axis=1)
    def blend(previous, rows_normed):
        base = rows_normed.astype(jnp.float32)
        delta = previous.astype(jnp.float32) - base
        return (base[None] + delta[None] * previous_item_mixers[:, None, :]).astype(jnp.bfloat16)

    def project(mixed):
        return (
            jnp.einsum(
                "itd,ide->ite", mixed[:4], mapping_matrices_pile, preferred_element_type=jnp.float32
            ),
            jnp.dot(mixed[4], fading_narrow_left, preferred_element_type=jnp.float32),
        )

    previous = jnp.concatenate([jnp.zeros_like(normed[:1]), normed[: rows - 1]], axis=0)
    previous = jnp.where(is_start[:, None], jnp.zeros_like(previous), previous)
    projected, lowrank = project(blend(previous, normed))
    edge = from_behind(normed[rows - 1 :], SEQ, 1)
    edge = jnp.where(is_start[0], jnp.zeros_like(edge), edge)
    edge_projected, edge_lowrank = project(blend(edge, normed[:1]))
    projected = lax.dynamic_update_slice(projected, edge_projected, (0, 0, 0))
    lowrank = lax.dynamic_update_slice(lowrank, edge_lowrank, (0, 0))
    recept = projected[0].astype(jnp.bfloat16)
    key_rows = projected[1].astype(jnp.bfloat16)
    value_rows = projected[2].astype(jnp.bfloat16)
    gate = jax.nn.silu(projected[3]).astype(jnp.bfloat16)
    lowrank_decay_delta = jnp.tanh(lowrank).astype(jnp.bfloat16)
    decay_logarithm = -feature_fading_baseline[None, :] * jnp.exp(
        jnp.dot(lowrank_decay_delta, fading_narrow_right, preferred_element_type=jnp.float32)
    )

    def split_heads(values):
        return (
            values.astype(jnp.float32)
            .reshape(blocks, block, mixing_values_divided, CHANNELS_ONE_HEAD)
            .transpose(0, 2, 1, 3)
        )

    inputs = (
        split_heads(recept),
        split_heads(key_rows),
        split_heads(value_rows),
        split_heads(decay_logarithm),
        segment.reshape(blocks, block),
        is_start.astype(jnp.float32).reshape(blocks, block),
    )
    order = jnp.arange(block)
    lower_incl = (order[None, :] <= order[:, None]).astype(jnp.float32)
    strictly = order[None, :] < order[:, None]
    diagonal_extra_contribution = diagonal_boost_coefficient.reshape(
        mixing_values_divided, CHANNELS_ONE_HEAD
    )

    gating_rows_tile, query_array_tile, content_slab, lw_b, seg_b, start_b = inputs
    incl = jnp.einsum("ts,bhsc->bhtc", lower_incl, lw_b, precision=highest)
    excl = incl - lw_b
    present_item_reward = jnp.sum(
        gating_rows_tile * diagonal_extra_contribution[None, :, None, :] * query_array_tile, axis=-1
    )
    seen = jnp.einsum("ts,bs->bt", lower_incl, start_b, precision=highest)
    valid = (seen == 0.0).astype(jnp.float32)
    carried = gating_rows_tile * jnp.exp(excl) * valid[:, None, :, None]
    total = incl[:, :, block - 1, :]
    keep = (seen[:, block - 1] == 0.0).astype(jnp.float32)
    tail_ok = (seg_b == seg_b[:, block - 1 :]).astype(jnp.float32)
    tail = query_array_tile * jnp.exp(total[:, :, None, :] - incl) * tail_ok[:, None, :, None]
    block_state = jnp.einsum("bhsc,bhsv->bhcv", tail, content_slab, precision=highest)
    block_decay = keep[:, None, None] * jnp.exp(total)

    state = jnp.zeros_like(block_state[0])
    offset = jnp.zeros_like(total[0])
    alive = jnp.float32(1.0)
    entering, reach = [], []
    for index in range(blocks):
        entering.append(state)
        reach.append(alive * jnp.exp(offset))
        state = block_decay[index][:, :, None] * state + block_state[index]
        offset = offset + total[index]
        alive = alive * keep[index]
    entering = jnp.stack(entering)
    from_start = carried * jnp.stack(reach)[:, :, None, :]
    end_state = state
    decay_total = alive * jnp.exp(offset)

    packed = jnp.concatenate([end_state, decay_total[:, None, :]], axis=1)

    def combine(received, own):
        own_state, own_decay = own[:, :CHANNELS_ONE_HEAD], own[:, CHANNELS_ONE_HEAD:]
        got_state, got_decay = received[:, :CHANNELS_ONE_HEAD], received[:, CHANNELS_ONE_HEAD:]
        state = jnp.transpose(own_decay, (0, 2, 1)) * got_state + own_state
        return jnp.concatenate([state, own_decay * got_decay], axis=1)

    devices = size_of(SEQ)
    def block_scores(index, incl_b, excl_b, recept_b, key_b):
        pair_ok = strictly & (seg_b[index][None, :] == seg_b[index][:, None])
        gap = jnp.minimum(excl_b[:, :, None, :] - incl_b[:, None, :, :], 0.0)
        weight = jnp.where(pair_ok[None, :, :, None], jnp.exp(gap), 0.0)
        return jnp.einsum("htc,hsc,htsc->hts", recept_b, key_b, weight, precision=highest)

    scores = []
    prefix = from_behind(packed, SEQ, 1)
    distance = 1
    while distance < devices:
        index = len(scores)
        if index < blocks:
            operands = (incl[index], excl[index], gating_rows_tile[index], query_array_tile[index])
            prefix, operands = lax.optimization_barrier((prefix, operands))
            scores.append(block_scores(index, *operands))
        prefix = combine(from_behind(prefix, SEQ, distance), prefix)
        distance *= 2
    for index in range(len(scores), blocks):
        scores.append(
            block_scores(index, incl[index], excl[index], gating_rows_tile[index], query_array_tile[index])
        )
    scores = jnp.stack(scores)
    outs = (
        jnp.einsum("bhts,bhsv->bhtv", scores, content_slab, precision=highest)
        + present_item_reward[..., None] * content_slab
        + jnp.einsum("bhtc,bhcv->bhtv", carried, entering, precision=highest)
    )
    incoming = prefix[:, :CHANNELS_ONE_HEAD]
    outs = outs + jnp.einsum("bhtc,hcv->bhtv", from_start, incoming, precision=highest)
    wkv = outs.transpose(0, 2, 1, 3).reshape(rows, mixing_values_divided, CHANNELS_ONE_HEAD)
    mean = jnp.mean(wkv, axis=-1, keepdims=True)
    centred = wkv - mean
    spread = jnp.mean(centred * centred, axis=-1, keepdims=True)
    grouped = (centred * lax.rsqrt(spread + 0.00064)).reshape(
        rows, local_width
    ) * cluster_standardize_scale + cluster_standardize_offset
    gated = (grouped * gate.astype(jnp.float32)).astype(jnp.bfloat16)
    partial_sum = jnp.dot(gated, emitted_mapping_matrix, preferred_element_type=jnp.float32)
    parts = lax.axis_size("tp")
    pieces = partial_sum.astype(jnp.bfloat16).reshape(rows, parts, local_width).transpose(1, 0, 2)
    pieces = lax.all_to_all(pieces, "tp", 0, 0, tiled=True)
    mine = jnp.sum(pieces.astype(jnp.float32), axis=0)
    return (tier_source_concatenated.astype(jnp.float32) + mine).astype(jnp.bfloat16)


def solution(mesh):
    groups = 8 if mesh.shape["seq"] % 8 == 0 else 1
    devices = mesh.devices.reshape(mesh.shape["seq"] // groups, groups, mesh.shape["tp"])
    mesh = jax.sharding.Mesh(devices, ("seq_hi", "seq_lo", "tp"))
    in_specs = (
        P(SEQ, "tp"),
        P(),
        P(),
        P(),
        P(),
        P(None, None, "tp"),
        P(),
        P(None, "tp"),
        P("tp"),
        P("tp"),
        P("tp"),
        P("tp"),
        P("tp", None),
    )
    out_specs = P(SEQ, "tp")
    return jax.shard_map(body, mesh=mesh, in_specs=in_specs, out_specs=out_specs, check_vma=False)
```

```python
import math

import jax
import jax.numpy as jnp
from jax import lax
from jax.sharding import PartitionSpec as P

CHANNELS_ONE_HEAD = 64


highest = lax.Precision.HIGHEST


SEQ = ("seq_hi", "seq_lo")


def size_of(axes):
    return math.prod(lax.axis_size(axis) for axis in axes)


def from_behind(block, axis, distance):
    devices = range(size_of(axis))
    route = [(i - distance, i) for i in devices if i - distance in devices]
    return lax.ppermute(block, axis, route)


def layer_norm(rows, gain, bias, eps):
    mean = jnp.mean(rows, axis=-1, keepdims=True)
    centred = rows - mean
    spread = jnp.mean(centred * centred, axis=-1, keepdims=True)
    return centred * lax.rsqrt(spread + eps) * gain + bias


def body(
    tier_source_concatenated,
    prompt_sizes_ordered,
    tier_standardize_scale,
    tier_standardize_offset,
    previous_item_mixers,
    mapping_matrices_pile,
    fading_narrow_left,
    fading_narrow_right,
    feature_fading_baseline,
    diagonal_boost_coefficient,
    cluster_standardize_scale,
    cluster_standardize_offset,
    emitted_mapping_matrix,
):
    rows = tier_source_concatenated.shape[0]
    local_width = mapping_matrices_pile.shape[2]
    mixing_values_divided = local_width // CHANNELS_ONE_HEAD
    block = min(32, rows)
    blocks = rows // block
    full = lax.all_gather(tier_source_concatenated, "tp", axis=1, tiled=True)
    normed = layer_norm(
        full.astype(jnp.float32), tier_standardize_scale, tier_standardize_offset, 1e-05
    ).astype(jnp.bfloat16)
    first = jnp.cumsum(prompt_sizes_ordered) - prompt_sizes_ordered
    position = lax.axis_index(SEQ) * rows + jnp.arange(rows, dtype=jnp.int32)
    is_start = jnp.any(position[:, None] == first[None, :], axis=1)
    segment = jnp.sum((first[None, :] <= position[:, None]).astype(jnp.int32), axis=1)
    def blend(previous, rows_normed):
        base = rows_normed.astype(jnp.float32)
        delta = previous.astype(jnp.float32) - base
        return (base[None] + delta[None] * previous_item_mixers[:, None, :]).astype(jnp.bfloat16)

    def project(mixed):
        return (
            jnp.einsum(
                "itd,ide->ite", mixed[:4], mapping_matrices_pile, preferred_element_type=jnp.float32
            ),
            jnp.dot(mixed[4], fading_narrow_left, preferred_element_type=jnp.float32),
        )

    previous = jnp.concatenate([jnp.zeros_like(normed[:1]), normed[: rows - 1]], axis=0)
    previous = jnp.where(is_start[:, None], jnp.zeros_like(previous), previous)
    projected, lowrank = project(blend(previous, normed))
    edge = from_behind(normed[rows - 1 :], SEQ, 1)
    edge = jnp.where(is_start[0], jnp.zeros_like(edge), edge)
    edge_projected, edge_lowrank = project(blend(edge, normed[:1]))
    projected = lax.dynamic_update_slice(projected, edge_projected, (0, 0, 0))
    lowrank = lax.dynamic_update_slice(lowrank, edge_lowrank, (0, 0))
    recept = projected[0].astype(jnp.bfloat16)
    key_rows = projected[1].astype(jnp.bfloat16)
    value_rows = projected[2].astype(jnp.bfloat16)
    gate = jax.nn.silu(projected[3]).astype(jnp.bfloat16)
    lowrank_decay_delta = jnp.tanh(lowrank).astype(jnp.bfloat16)
    decay_logarithm = -feature_fading_baseline[None, :] * jnp.exp(
        jnp.dot(lowrank_decay_delta, fading_narrow_right, preferred_element_type=jnp.float32)
    )

    def split_heads(values):
        return (
            values.astype(jnp.float32)
            .reshape(blocks, block, mixing_values_divided, CHANNELS_ONE_HEAD)
            .transpose(0, 2, 1, 3)
        )

    inputs = (
        split_heads(recept),
        split_heads(key_rows),
        split_heads(value_rows),
        split_heads(decay_logarithm),
        segment.reshape(blocks, block),
        is_start.astype(jnp.float32).reshape(blocks, block),
    )
    order = jnp.arange(block)
    lower_incl = (order[None, :] <= order[:, None]).astype(jnp.float32)
    strictly = order[None, :] < order[:, None]
    diagonal_extra_contribution = diagonal_boost_coefficient.reshape(
        mixing_values_divided, CHANNELS_ONE_HEAD
    )

    gating_rows_tile, query_array_tile, content_slab, lw_b, seg_b, start_b = inputs
    incl = jnp.einsum("ts,bhsc->bhtc", lower_incl, lw_b, precision=highest)
    excl = incl - lw_b
    present_item_reward = jnp.sum(
        gating_rows_tile * diagonal_extra_contribution[None, :, None, :] * query_array_tile, axis=-1
    )
    seen = jnp.einsum("ts,bs->bt", lower_incl, start_b, precision=highest)
    valid = (seen == 0.0).astype(jnp.float32)
    carried = gating_rows_tile * jnp.exp(excl) * valid[:, None, :, None]
    total = incl[:, :, block - 1, :]
    keep = (seen[:, block - 1] == 0.0).astype(jnp.float32)
    tail_ok = (seg_b == seg_b[:, block - 1 :]).astype(jnp.float32)
    tail = query_array_tile * jnp.exp(total[:, :, None, :] - incl) * tail_ok[:, None, :, None]
    block_state = jnp.einsum("bhsc,bhsv->bhcv", tail, content_slab, precision=highest)
    block_decay = keep[:, None, None] * jnp.exp(total)

    state = jnp.zeros_like(block_state[0])
    offset = jnp.zeros_like(total[0])
    alive = jnp.float32(1.0)
    entering, reach = [], []
    for index in range(blocks):
        entering.append(state)
        reach.append(alive * jnp.exp(offset))
        state = block_decay[index][:, :, None] * state + block_state[index]
        offset = offset + total[index]
        alive = alive * keep[index]
    entering = jnp.stack(entering)
    from_start = carried * jnp.stack(reach)[:, :, None, :]
    end_state = state
    decay_total = alive * jnp.exp(offset)

    packed = jnp.concatenate([end_state, decay_total[:, None, :]], axis=1)

    def combine(received, own):
        own_state, own_decay = own[:, :CHANNELS_ONE_HEAD], own[:, CHANNELS_ONE_HEAD:]
        got_state, got_decay = received[:, :CHANNELS_ONE_HEAD], received[:, CHANNELS_ONE_HEAD:]
        state = jnp.transpose(own_decay, (0, 2, 1)) * got_state + own_state
        return jnp.concatenate([state, own_decay * got_decay], axis=1)

    devices = size_of(SEQ)
    def block_scores(index, incl_b, excl_b, recept_b, key_b):
        pair_ok = strictly & (seg_b[index][None, :] == seg_b[index][:, None])
        gap = jnp.minimum(excl_b[:, :, None, :] - incl_b[:, None, :, :], 0.0)
        weight = jnp.where(pair_ok[None, :, :, None], jnp.exp(gap), 0.0)
        return jnp.einsum("htc,hsc,htsc->hts", recept_b, key_b, weight, precision=highest)

    scores = []
    prefix = from_behind(packed, SEQ, 1)
    distance = 1
    while distance < devices:
        prefix = combine(from_behind(prefix, SEQ, distance), prefix)
        distance *= 2
        index = len(scores)
        if index < blocks and distance > 2:
            operands = (incl[index], excl[index], gating_rows_tile[index], query_array_tile[index])
            prefix, operands = lax.optimization_barrier((prefix, operands))
            scores.append(block_scores(index, *operands))
    for index in range(len(scores), blocks):
        scores.append(
            block_scores(index, incl[index], excl[index], gating_rows_tile[index], query_array_tile[index])
        )
    scores = jnp.stack(scores)
    outs = (
        jnp.einsum("bhts,bhsv->bhtv", scores, content_slab, precision=highest)
        + present_item_reward[..., None] * content_slab
        + jnp.einsum("bhtc,bhcv->bhtv", carried, entering, precision=highest)
    )
    incoming = prefix[:, :CHANNELS_ONE_HEAD]
    outs = outs + jnp.einsum("bhtc,hcv->bhtv", from_start, incoming, precision=highest)
    wkv = outs.transpose(0, 2, 1, 3).reshape(rows, mixing_values_divided, CHANNELS_ONE_HEAD)
    mean = jnp.mean(wkv, axis=-1, keepdims=True)
    centred = wkv - mean
    spread = jnp.mean(centred * centred, axis=-1, keepdims=True)
    grouped = (centred * lax.rsqrt(spread + 0.00064)).reshape(
        rows, local_width
    ) * cluster_standardize_scale + cluster_standardize_offset
    gated = (grouped * gate.astype(jnp.float32)).astype(jnp.bfloat16)
    partial_sum = jnp.dot(gated, emitted_mapping_matrix, preferred_element_type=jnp.float32)
    parts = lax.axis_size("tp")
    pieces = partial_sum.astype(jnp.bfloat16).reshape(rows, parts, local_width).transpose(1, 0, 2)
    pieces = lax.all_to_all(pieces, "tp", 0, 0, tiled=True)
    mine = jnp.sum(pieces.astype(jnp.float32), axis=0)
    return (tier_source_concatenated.astype(jnp.float32) + mine).astype(jnp.bfloat16)


def solution(mesh):
    groups = 8 if mesh.shape["seq"] % 8 == 0 else 1
    devices = mesh.devices.reshape(mesh.shape["seq"] // groups, groups, mesh.shape["tp"])
    mesh = jax.sharding.Mesh(devices, ("seq_hi", "seq_lo", "tp"))
    in_specs = (
        P(SEQ, "tp"),
        P(),
        P(),
        P(),
        P(),
        P(None, None, "tp"),
        P(),
        P(None, "tp"),
        P("tp"),
        P("tp"),
        P("tp"),
        P("tp"),
        P("tp", None),
    )
    out_specs = P(SEQ, "tp")
    return jax.shard_map(body, mesh=mesh, in_specs=in_specs, out_specs=out_specs, check_vma=False)
```

```python
import math

import jax
import jax.numpy as jnp
from jax import lax
from jax.sharding import PartitionSpec as P

CHANNELS_ONE_HEAD = 64


highest = lax.Precision.HIGHEST


SEQ = ("seq_hi", "seq_lo")


def size_of(axes):
    return math.prod(lax.axis_size(axis) for axis in axes)


def from_behind(block, axis, distance):
    devices = range(size_of(axis))
    route = [(i - distance, i) for i in devices if i - distance in devices]
    return lax.ppermute(block, axis, route)


def layer_norm(rows, gain, bias, eps):
    mean = jnp.mean(rows, axis=-1, keepdims=True)
    centred = rows - mean
    spread = jnp.mean(centred * centred, axis=-1, keepdims=True)
    return centred * lax.rsqrt(spread + eps) * gain + bias


def body(
    tier_source_concatenated,
    prompt_sizes_ordered,
    tier_standardize_scale,
    tier_standardize_offset,
    previous_item_mixers,
    mapping_matrices_pile,
    fading_narrow_left,
    fading_narrow_right,
    feature_fading_baseline,
    diagonal_boost_coefficient,
    cluster_standardize_scale,
    cluster_standardize_offset,
    emitted_mapping_matrix,
):
    rows = tier_source_concatenated.shape[0]
    local_width = mapping_matrices_pile.shape[2]
    mixing_values_divided = local_width // CHANNELS_ONE_HEAD
    block = min(32, rows)
    blocks = rows // block
    full = lax.all_gather(tier_source_concatenated, "tp", axis=1, tiled=True)
    normed = layer_norm(
        full.astype(jnp.float32), tier_standardize_scale, tier_standardize_offset, 1e-05
    ).astype(jnp.bfloat16)
    first = jnp.cumsum(prompt_sizes_ordered) - prompt_sizes_ordered
    position = lax.axis_index(SEQ) * rows + jnp.arange(rows, dtype=jnp.int32)
    is_start = jnp.any(position[:, None] == first[None, :], axis=1)
    segment = jnp.sum((first[None, :] <= position[:, None]).astype(jnp.int32), axis=1)
    def blend(previous, rows_normed):
        base = rows_normed.astype(jnp.float32)
        delta = previous.astype(jnp.float32) - base
        return (base[None] + delta[None] * previous_item_mixers[:, None, :]).astype(jnp.bfloat16)

    def project(mixed):
        return (
            jnp.einsum(
                "itd,ide->ite", mixed[:4], mapping_matrices_pile, preferred_element_type=jnp.float32
            ),
            jnp.dot(mixed[4], fading_narrow_left, preferred_element_type=jnp.float32),
        )

    previous = jnp.concatenate([jnp.zeros_like(normed[:1]), normed[: rows - 1]], axis=0)
    previous = jnp.where(is_start[:, None], jnp.zeros_like(previous), previous)
    projected, lowrank = project(blend(previous, normed))
    edge = from_behind(normed[rows - 1 :], SEQ, 1)
    edge = jnp.where(is_start[0], jnp.zeros_like(edge), edge)
    edge_projected, edge_lowrank = project(blend(edge, normed[:1]))
    projected = lax.dynamic_update_slice(projected, edge_projected, (0, 0, 0))
    lowrank = lax.dynamic_update_slice(lowrank, edge_lowrank, (0, 0))
    recept = projected[0].astype(jnp.bfloat16)
    key_rows = projected[1].astype(jnp.bfloat16)
    value_rows = projected[2].astype(jnp.bfloat16)
    gate = jax.nn.silu(projected[3]).astype(jnp.bfloat16)
    lowrank_decay_delta = jnp.tanh(lowrank).astype(jnp.bfloat16)
    decay_logarithm = -feature_fading_baseline[None, :] * jnp.exp(
        jnp.dot(lowrank_decay_delta, fading_narrow_right, preferred_element_type=jnp.float32)
    )

    def split_heads(values):
        return (
            values.astype(jnp.float32)
            .reshape(blocks, block, mixing_values_divided, CHANNELS_ONE_HEAD)
            .transpose(0, 2, 1, 3)
        )

    inputs = (
        split_heads(recept),
        split_heads(key_rows),
        split_heads(value_rows),
        split_heads(decay_logarithm),
        segment.reshape(blocks, block),
        is_start.astype(jnp.float32).reshape(blocks, block),
    )
    order = jnp.arange(block)
    lower_incl = (order[None, :] <= order[:, None]).astype(jnp.float32)
    strictly = order[None, :] < order[:, None]
    diagonal_extra_contribution = diagonal_boost_coefficient.reshape(
        mixing_values_divided, CHANNELS_ONE_HEAD
    )

    gating_rows_tile, query_array_tile, content_slab, lw_b, seg_b, start_b = inputs
    incl = jnp.einsum("ts,bhsc->bhtc", lower_incl, lw_b, precision=highest)
    excl = incl - lw_b
    present_item_reward = jnp.sum(
        gating_rows_tile * diagonal_extra_contribution[None, :, None, :] * query_array_tile, axis=-1
    )
    seen = jnp.einsum("ts,bs->bt", lower_incl, start_b, precision=highest)
    valid = (seen == 0.0).astype(jnp.float32)
    carried = gating_rows_tile * jnp.exp(excl) * valid[:, None, :, None]
    total = incl[:, :, block - 1, :]
    keep = (seen[:, block - 1] == 0.0).astype(jnp.float32)
    tail_ok = (seg_b == seg_b[:, block - 1 :]).astype(jnp.float32)
    tail = query_array_tile * jnp.exp(total[:, :, None, :] - incl) * tail_ok[:, None, :, None]
    block_state = jnp.einsum("bhsc,bhsv->bhcv", tail, content_slab, precision=highest)
    block_decay = keep[:, None, None] * jnp.exp(total)

    state = jnp.zeros_like(block_state[0])
    offset = jnp.zeros_like(total[0])
    alive = jnp.float32(1.0)
    entering, reach = [], []
    for index in range(blocks):
        entering.append(state)
        reach.append(alive * jnp.exp(offset))
        state = block_decay[index][:, :, None] * state + block_state[index]
        offset = offset + total[index]
        alive = alive * keep[index]
    entering = jnp.stack(entering)
    from_start = carried * jnp.stack(reach)[:, :, None, :]
    end_state = state
    decay_total = alive * jnp.exp(offset)

    packed = jnp.concatenate([end_state, decay_total[:, None, :]], axis=1)

    def combine(received, own):
        own_state, own_decay = own[:, :CHANNELS_ONE_HEAD], own[:, CHANNELS_ONE_HEAD:]
        got_state, got_decay = received[:, :CHANNELS_ONE_HEAD], received[:, CHANNELS_ONE_HEAD:]
        state = jnp.transpose(own_decay, (0, 2, 1)) * got_state + own_state
        return jnp.concatenate([state, own_decay * got_decay], axis=1)

    devices = size_of(SEQ)
    def block_scores(index, incl_b, excl_b, recept_b, key_b):
        pair_ok = strictly & (seg_b[index][None, :] == seg_b[index][:, None])
        gap = jnp.minimum(excl_b[:, :, None, :] - incl_b[:, None, :, :], 0.0)
        weight = jnp.where(pair_ok[None, :, :, None], jnp.exp(gap), 0.0)
        return jnp.einsum("htc,hsc,htsc->hts", recept_b, key_b, weight, precision=highest)

    scores = [block_scores(0, incl[0], excl[0], gating_rows_tile[0], query_array_tile[0])]
    prefix = from_behind(packed, SEQ, 1)
    distance = 1
    while distance < devices:
        prefix = combine(from_behind(prefix, SEQ, distance), prefix)
        distance *= 2
        index = len(scores)
        if index < blocks and distance > 2:
            operands = (incl[index], excl[index], gating_rows_tile[index], query_array_tile[index])
            prefix, operands = lax.optimization_barrier((prefix, operands))
            scores.append(block_scores(index, *operands))
    for index in range(len(scores), blocks):
        scores.append(
            block_scores(index, incl[index], excl[index], gating_rows_tile[index], query_array_tile[index])
        )
    scores = jnp.stack(scores)
    outs = (
        jnp.einsum("bhts,bhsv->bhtv", scores, content_slab, precision=highest)
        + present_item_reward[..., None] * content_slab
        + jnp.einsum("bhtc,bhcv->bhtv", carried, entering, precision=highest)
    )
    incoming = prefix[:, :CHANNELS_ONE_HEAD]
    outs = outs + jnp.einsum("bhtc,hcv->bhtv", from_start, incoming, precision=highest)
    wkv = outs.transpose(0, 2, 1, 3).reshape(rows, mixing_values_divided, CHANNELS_ONE_HEAD)
    mean = jnp.mean(wkv, axis=-1, keepdims=True)
    centred = wkv - mean
    spread = jnp.mean(centred * centred, axis=-1, keepdims=True)
    grouped = (centred * lax.rsqrt(spread + 0.00064)).reshape(
        rows, local_width
    ) * cluster_standardize_scale + cluster_standardize_offset
    gated = (grouped * gate.astype(jnp.float32)).astype(jnp.bfloat16)
    partial_sum = jnp.dot(gated, emitted_mapping_matrix, preferred_element_type=jnp.float32)
    parts = lax.axis_size("tp")
    pieces = partial_sum.astype(jnp.bfloat16).reshape(rows, parts, local_width).transpose(1, 0, 2)
    pieces = lax.all_to_all(pieces, "tp", 0, 0, tiled=True)
    mine = jnp.sum(pieces.astype(jnp.float32), axis=0)
    return (tier_source_concatenated.astype(jnp.float32) + mine).astype(jnp.bfloat16)


def solution(mesh):
    groups = 8 if mesh.shape["seq"] % 8 == 0 else 1
    devices = mesh.devices.reshape(mesh.shape["seq"] // groups, groups, mesh.shape["tp"])
    mesh = jax.sharding.Mesh(devices, ("seq_hi", "seq_lo", "tp"))
    in_specs = (
        P(SEQ, "tp"),
        P(),
        P(),
        P(),
        P(),
        P(None, None, "tp"),
        P(),
        P(None, "tp"),
        P("tp"),
        P("tp"),
        P("tp"),
        P("tp"),
        P("tp", None),
    )
    out_specs = P(SEQ, "tp")
    return jax.shard_map(body, mesh=mesh, in_specs=in_specs, out_specs=out_specs, check_vma=False)
```
